128 devices in a mesh: req: 4 (over y), head: 32 (over x, z, core).
Axes of the slice: x: 4, y: 4, z: 4, core: 2. Of those that a mesh axis runs over, the one named last changes fastest.
Arguments:
- hidden_in: bfloat16 [8192, 2048], P(('req', 'head')), may hold values from -6 to 6
- queries: bfloat16 [8192, 2048], P(('req', 'head')), may hold values from -160 to 160
- keys_values: bfloat16 [8192, 1024], P(('req', 'head')), may hold values from -10 to 10
- request_of_row: int32 [8192], P('req'), may hold values from 0 to 7, as said below
- page_route: int32 [4, 32, 4], P('req', 'head'), may hold values from 0 to 3, each once within a row
- expert_ids: int32 [8192, 6], P(('req', 'head')), may hold values from 0 to 31, all different within a row; in each aligned block of 64 rows (0 to 63, 64 to 127, ...) at most 14 rows name the same one
- expert_weights: float32 [8192, 6], P(('req', 'head')), may hold values from 0.05 to 0.5
- norm_gain: float32 [2048], replicated, may hold values from 0.25 to 1.75
- shared_gate_up: bfloat16 [2048, 2, 1408], replicated, may hold values from -0.125 to 0.125
- shared_down: bfloat16 [1408, 2048], replicated, may hold values from -0.15625 to 0.15625
- expert_gate_up: bfloat16 [32, 2, 1408, 2048], P('head', None, 'req'), may hold values from -0.125 to 0.125
- expert_down: bfloat16 [32, 1408, 2048], P('head', 'req'), may hold values from -0.15625 to 0.15625
Outputs:
- layer_out: bfloat16 [8192, 2048], P(('req', 'head'))
The draws below stay inside these ranges and needn't reach their ends.
Inputs may be any that keep to these rules, and one draw needn't show every extreme that they name: `request_of_row`: each group of 2048 rows g holds two requests, ids 2 g then 2 g + 1, each a whole number of pages of 16 rows and at least 128 rows long. `page_route`: for every device, the groups receiving its pages form a permutation of all groups. `expert_ids`: each row names 6 different experts; among the rows of one device no expert is named more than 14 times, and some device names some expert exactly 14 times.
All inputs are finite; a program needn't handle non-finite values.
Results may differ from the reference program's by a relative error of at most 0.006.
Values may be sent and summed in bfloat16 or wider, within the bound.
No kernel may reach another device: no remote copies, remote signals or barrier semaphores. Data moves between devices by JAX's collectives and lax.ppermute only.
A program may use at most 192 MiB of HBM per device.

```python
import math
import jax
import jax.numpy as jnp
import numpy as np
from jax import lax

D = 2048
QUERY_HEADS = 16
KEY_VALUE_HEADS = 4
HEAD_SIZE = 128
FF = 1408
SFF = 1408
EXPERTS = 32
TOP = 6
TOK_DEV = 64
PAGE = 16
CAP = 14
GROUP_TOKENS = 2048
TOKEN_TOTAL = 8192
N_REQ = 4
N_HEAD = 32


def attention_inputs(key):
    query_key = jax.random.fold_in(key, 101)
    pair_random_key = jax.random.fold_in(key, 102)
    query_draw = jnp.clip(jax.random.normal(query_key, (TOKEN_TOTAL, QUERY_HEADS * HEAD_SIZE), jnp.float32), -6.0, 6.0)
    pair_sample = jnp.clip(jax.random.normal(pair_random_key, (TOKEN_TOTAL, 2 * KEY_VALUE_HEADS * HEAD_SIZE), jnp.float32), -6.0, 6.0)
    return (query_draw, pair_sample)


def draw_queries(key, part):
    return attention_inputs(key)[0].astype(jnp.bfloat16)


def draw_keys_values(key, part):
    return attention_inputs(key)[1].astype(jnp.bfloat16)


def draw_request_of_row(key, part):
    pages_group = GROUP_TOKENS // PAGE
    split_page = jax.random.randint(jax.random.fold_in(key, 105), (TOKEN_TOTAL // GROUP_TOKENS, 1), pages_group // 16, pages_group - pages_group // 16 + 1)
    page_index = jnp.arange(GROUP_TOKENS, dtype=jnp.int32)[None, :] // PAGE
    group_index = jnp.arange(TOKEN_TOTAL // GROUP_TOKENS, dtype=jnp.int32)[:, None]
    return (2 * group_index + (page_index >= split_page).astype(jnp.int32)).reshape(TOKEN_TOTAL).astype(jnp.int32)


def block_levels(stream_key, dims, cuts, smallest, high):
    def one(dim, blocks):
        heights = jax.random.uniform(jax.random.fold_in(jax.random.fold_in(stream_key, 6), dim), (blocks,), jnp.float32, smallest / len(cuts), high / len(cuts))
        return jnp.repeat(jnp.exp(heights), dims[dim] // blocks).reshape((-1,) + (1,) * (len(dims) - dim - 1))

    level = one(*cuts[0])
    for cut in cuts[1:]:
        level = level * one(*cut)
    return level


def routed_block(key, own, number, rows, amount, top, bound, lean):
    sequence = jax.random.permutation(key, amount)
    heavy_load, ordinary = shares(amount, rows * top, bound, lean, True), shares(amount, rows * top, bound, lean, False)
    places = jnp.arange(amount)

    def named(tallies, offset_by):
        used = int((tallies > 0).sum())
        fixed = max(1, used // 4)
        shifted = fixed + (places - fixed + offset_by * (used - fixed)) % max(1, amount - fixed)
        return jnp.zeros((amount,), jnp.int32).at[sequence[jnp.where(places < fixed, places, shifted)]].set(jnp.asarray(tallies, jnp.int32))

    tallies = jnp.where(number % 4 == 0, named(heavy_load, number // 4), named(ordinary, number - number // 4 - 1))
    mixed = jax.random.permutation(jax.random.fold_in(own, 3), amount)
    giver, sink = mixed[0:amount // 2 * 2:2], mixed[1:amount // 2 * 2:2]
    room = jnp.minimum(tallies[giver] - 1, bound - tallies[sink]) // 2
    room = jnp.where((giver == sequence[0]) | (sink == sequence[0]) | (tallies[sink] == 0), 0, jnp.maximum(room, 0))
    shifted = jax.random.randint(jax.random.fold_in(own, 4), (amount // 2,), 0, 1 << 20) % (room + 1)
    tallies = tallies.at[giver].add(-shifted).at[sink].add(shifted)
    members = jnp.searchsorted(jnp.cumsum(tallies), jnp.arange(rows * top), side="right").astype(jnp.int32)
    listing = members.reshape(top, rows).T
    listing = listing[jax.random.permutation(jax.random.fold_in(own, 1), rows)]
    offset_by = jax.random.randint(jax.random.fold_in(own, 2), (rows, 1), 0, top)
    return jnp.take_along_axis(listing, (jnp.arange(top)[None, :] + offset_by) % top, axis=1)


def shares(count, total, limit, slope, full):
    loads = [(1 << 20) // math.isqrt(standing ** slope) + 1 for standing in range(1, count + 1)]
    largest = limit if full else min(limit, max(-(-total // count), total * loads[0] // sum(loads)))
    least = 1 if total - largest >= count - 1 else 0
    given, rest = [largest] + [least] * (count - 1), total - largest - least * (count - 1)
    while rest > 0:
        candidates = [i for i in range(1, count) if given[i] < largest] or [i for i in range(1, count) if given[i] < limit]
        mass, budget = sum([loads[i] for i in candidates]), rest
        for i in candidates:
            addition = min(limit - given[i], max(1, budget * loads[i] // mass), rest)
            given[i] = given[i] + addition
            rest = rest - addition
    return np.array(given)


def gaussian(own_key, extent, scale, reach, shards=(), kind=jnp.bfloat16):
    entries = scale * jax.random.normal(own_key, extent, jnp.float32)
    if shards:
        entries = entries * block_levels(own_key, extent, shards, -0.22, 0.18)
    return jnp.clip(entries, -reach, reach).astype(kind)


def setup_inputs(seed: int = 0) -> dict:
    streams_of = jax.random.split(jax.random.key(seed), 13)
    hidden_in = gaussian(streams_of[0], (TOKEN_TOTAL, D), 1.0, 6.0, ((0, 128),))
    queries = draw_queries(jax.random.fold_in(streams_of[12], 71), 0)
    keys_values = draw_keys_values(jax.random.fold_in(streams_of[12], 71), 0)
    request_of_row = draw_request_of_row(jax.random.fold_in(streams_of[12], 71), 0)
    page_route = jax.vmap(lambda own: jax.random.permutation(own, N_REQ))(jax.random.split(streams_of[4], N_REQ * N_HEAD)).reshape((N_REQ, N_HEAD, N_REQ)).astype(jnp.int32)
    expert_ids_keys = jax.random.split(jax.random.fold_in(streams_of[5], 1), TOKEN_TOTAL // TOK_DEV)
    expert_ids_turns = jax.random.permutation(jax.random.fold_in(streams_of[5], 3), TOKEN_TOTAL // TOK_DEV)
    expert_ids = jax.vmap(lambda own, number: routed_block(jax.random.fold_in(streams_of[5], 2), own, number, TOK_DEV, EXPERTS, TOP, CAP, 1))(expert_ids_keys, expert_ids_turns).reshape((TOKEN_TOTAL, TOP))
    expert_weights = jnp.clip(jnp.exp(math.log(0.5) - 2.3025851 * jax.random.uniform(streams_of[6], (TOKEN_TOTAL, TOP), jnp.float32) ** block_levels(streams_of[6], (TOKEN_TOTAL, TOP), ((0, 128),), -0.2, 0.2)), 0.05, 0.5)
    norm_gain = jnp.clip(1.0 + 0.15 * jax.random.normal(streams_of[7], (D,), jnp.float32), 0.25, 1.75)
    shared_gate_up = gaussian(streams_of[8], (D, 2, SFF), D ** -0.5, 0.125)
    shared_down = gaussian(streams_of[9], (SFF, D), SFF ** -0.5, 0.15625)
    expert_gate_up = gaussian(streams_of[10], (EXPERTS, 2, FF, D), D ** -0.5, 0.125, ((0, 32), (2, 4)))
    expert_down = gaussian(streams_of[11], (EXPERTS, FF, D), FF ** -0.5, 0.15625, ((0, 32), (1, 4)))
    return {"hidden_in": hidden_in, "queries": queries, "keys_values": keys_values, "request_of_row": request_of_row, "page_route": page_route, "expert_ids": expert_ids, "expert_weights": expert_weights, "norm_gain": norm_gain, "shared_gate_up": shared_gate_up, "shared_down": shared_down, "expert_gate_up": expert_gate_up, "expert_down": expert_down}


negative_large = -1e+30

def silu_mul(gate_value, upward):
    return gate_value / (1.0 + jnp.exp(-gate_value)) * upward

def source_rows(page_route):
    rows_all = jnp.arange(TOKEN_TOTAL, dtype=jnp.int32)
    group_of = rows_all // GROUP_TOKENS
    column_of = rows_all // TOK_DEV % N_HEAD
    page_slot = rows_all % TOK_DEV // PAGE
    within_page = rows_all % PAGE
    targets = page_route[page_slot, column_of]
    matches = (targets == group_of[:, None]).astype(jnp.int32)
    source_page = lax.optimization_barrier(jnp.sum(matches * jnp.arange(N_REQ, dtype=jnp.int32)[None, :], axis=1))
    return ((page_slot * N_HEAD + column_of) * TOK_DEV + source_page * PAGE + within_page).astype(jnp.int32)

def attend_group(inputs):
    query_group, group_of_pair, segment_group = inputs
    position = jnp.arange(GROUP_TOKENS, dtype=jnp.int32)
    allowed = (segment_group[:, None] == segment_group[None, :]) & (position[None, :] <= position[:, None])
    group_fraction = QUERY_HEADS // KEY_VALUE_HEADS
    score_scale = HEAD_SIZE ** (-0.5)

    def one_head(head_index):
        query_head = lax.dynamic_slice_in_dim(query_group, head_index * HEAD_SIZE, HEAD_SIZE, 1)
        index_of_pair = head_index // group_fraction
        key_head = lax.dynamic_slice_in_dim(group_of_pair, index_of_pair * HEAD_SIZE, HEAD_SIZE, 1)
        head_values = lax.dynamic_slice_in_dim(group_of_pair, KEY_VALUE_HEADS * HEAD_SIZE + index_of_pair * HEAD_SIZE, HEAD_SIZE, 1)
        score = jnp.dot(query_head, key_head.T, preferred_element_type=jnp.float32) * score_scale
        masked = jnp.where(allowed, score, negative_large)
        top_score = lax.optimization_barrier(jnp.max(masked, axis=1, keepdims=True))
        weights = jnp.where(allowed, jnp.exp(masked - top_score), 0.0)
        row_total = lax.optimization_barrier(jnp.sum(weights, axis=1, keepdims=True))
        return jnp.dot(weights.astype(jnp.bfloat16), head_values, preferred_element_type=jnp.float32) / row_total
    heads_out = lax.map(one_head, jnp.arange(QUERY_HEADS, dtype=jnp.int32))
    return jnp.transpose(heads_out, (1, 0, 2)).reshape(GROUP_TOKENS, QUERY_HEADS * HEAD_SIZE)

def reference(hidden_in, queries, keys_values, request_of_row, page_route, expert_ids, expert_weights, norm_gain, shared_gate_up, shared_down, expert_gate_up, expert_down):
    source = source_rows(page_route)
    resid = jnp.take(hidden_in, source, axis=0)
    rows_of_queries = jnp.take(queries, source, axis=0)
    key_value_rows = jnp.take(keys_values, source, axis=0)
    grouped_rows = (rows_of_queries.reshape(N_REQ, GROUP_TOKENS, QUERY_HEADS * HEAD_SIZE), key_value_rows.reshape(N_REQ, GROUP_TOKENS, 2 * KEY_VALUE_HEADS * HEAD_SIZE), request_of_row.reshape(N_REQ, GROUP_TOKENS))
    context = lax.map(attend_group, grouped_rows).reshape(TOKEN_TOTAL, QUERY_HEADS * HEAD_SIZE)
    mixed_rows = resid.astype(jnp.float32) + context
    mean_square = lax.optimization_barrier(jnp.mean(mixed_rows * mixed_rows, axis=1, keepdims=True))
    normed = (mixed_rows * lax.rsqrt(mean_square + 1e-06) * norm_gain).astype(jnp.bfloat16)
    shared_both = jnp.dot(normed, shared_gate_up.reshape(D, 2 * SFF), preferred_element_type=jnp.float32).reshape(TOKEN_TOTAL, 2, SFF)
    shared_hidden = silu_mul(shared_both[:, 0], shared_both[:, 1]).astype(jnp.bfloat16)
    shared_out = jnp.dot(shared_hidden, shared_down, preferred_element_type=jnp.float32)
    flat_experts = expert_ids.reshape(-1)
    flat_weights = expert_weights.reshape(-1)
    most_rows = N_REQ * N_HEAD * CAP
    part_width = FF // N_REQ

    def one_expert(routed, expert):
        hit_mask = flat_experts == expert
        index_of_pair = jnp.nonzero(hit_mask, size=most_rows, fill_value=0)[0].astype(jnp.int32)
        live_rows = jnp.arange(most_rows, dtype=jnp.int32) < jnp.sum(hit_mask.astype(jnp.int32))
        token_of = (index_of_pair // TOP).astype(jnp.int32)
        rows_in = jnp.take(normed, token_of, axis=0)
        gate_up = lax.dynamic_index_in_dim(expert_gate_up, expert, 0, keepdims=False)
        down_matrix = lax.dynamic_index_in_dim(expert_down, expert, 0, keepdims=False)
        gate_value = jnp.dot(rows_in, gate_up[0].T, preferred_element_type=jnp.float32)
        upward = jnp.dot(rows_in, gate_up[1].T, preferred_element_type=jnp.float32)
        hidden = silu_mul(gate_value, upward).astype(jnp.bfloat16)
        result = jnp.zeros((most_rows, D), jnp.float32)
        for quarter in range(N_REQ):
            part_out = jnp.dot(hidden[:, quarter * part_width:(quarter + 1) * part_width], down_matrix[quarter * part_width:(quarter + 1) * part_width], preferred_element_type=jnp.float32).astype(jnp.bfloat16)
            result = result + lax.optimization_barrier(part_out).astype(jnp.float32)
        scaled = result * jnp.where(live_rows, jnp.take(flat_weights, index_of_pair), 0.0)[:, None]
        return (routed.at[token_of].add(scaled), None)
    routed = lax.scan(one_expert, jnp.zeros((TOKEN_TOTAL, D), jnp.float32), jnp.arange(EXPERTS, dtype=jnp.int32))[0]
    return (mixed_rows + shared_out + routed).astype(jnp.bfloat16)
```

```python
import jax
import jax.numpy as jnp
from jax import lax
from jax.sharding import PartitionSpec as P

QUERY_HEADS = 16
KEY_VALUE_HEADS = 4
HEAD_SIZE = 128
EXPERTS = 32
TOP = 6
CAP = 14


negative_large = -1e30


def silu_mul(gate_value, upward):
    return gate_value / (1.0 + jnp.exp(-gate_value)) * upward


def body(
    hidden_in,
    queries,
    keys_values,
    request_of_row,
    page_route,
    expert_ids,
    expert_weights,
    norm_gain,
    shared_gate_up,
    shared_down,
    expert_gate_up,
    expert_down,
):
    groups = lax.axis_size("req")
    columns = lax.axis_size("head")
    token_rows = hidden_in.shape[0]
    model_width = hidden_in.shape[1]
    page_rows = token_rows // groups
    group_ids = jnp.arange(groups, dtype=jnp.int32)
    page_dest = page_route.reshape(groups)
    matches = (page_dest[None, :] == group_ids[:, None]).astype(jnp.int32)
    dest_order = jnp.sum(matches * group_ids[None, :], axis=1)

    def by_dest(array_in):
        return jnp.take(array_in.reshape(groups, page_rows, array_in.shape[1]), dest_order, axis=0)

    widths = (hidden_in.shape[1], queries.shape[1], keys_values.shape[1])
    packed = jnp.concatenate((hidden_in, queries, keys_values), axis=1)
    moved = lax.all_to_all(by_dest(packed), "req", split_axis=0, concat_axis=0, tiled=True)
    moved = moved.reshape(token_rows, sum(widths))
    resid = moved[:, : widths[0]]
    rows_of_queries = moved[:, widths[0] : widths[0] + widths[1]]
    key_value_rows = moved[:, widths[0] + widths[1] :]
    group_fraction = QUERY_HEADS // KEY_VALUE_HEADS
    key_value_width = KEY_VALUE_HEADS * HEAD_SIZE
    score_scale = HEAD_SIZE ** (-0.5)
    query_start = lax.axis_index("head") * token_rows
    segment_query = lax.dynamic_slice_in_dim(request_of_row, query_start, token_rows)
    position_query = query_start + jnp.arange(token_rows, dtype=jnp.int32)
    query_fourfold = rows_of_queries.reshape(token_rows, KEY_VALUE_HEADS, group_fraction, HEAD_SIZE)
    start_state = (
        jnp.full((KEY_VALUE_HEADS, group_fraction, token_rows), negative_large, jnp.float32),
        jnp.zeros((KEY_VALUE_HEADS, group_fraction, token_rows), jnp.float32),
        jnp.zeros((KEY_VALUE_HEADS, group_fraction, token_rows, HEAD_SIZE), jnp.float32),
    )
    kv_piece = lax.all_gather(key_value_rows, "head", axis=0, tiled=True)
    piece_rows = kv_piece.shape[0]
    rows_per_block = 512

    def one_block(block_index, carried_block):
        offset = block_index * rows_per_block
        current_block = lax.dynamic_slice_in_dim(kv_piece, offset, rows_per_block)
        block_keys = current_block[:, :key_value_width].reshape(
            rows_per_block, KEY_VALUE_HEADS, HEAD_SIZE
        )
        block_values = current_block[:, key_value_width:].reshape(
            rows_per_block, KEY_VALUE_HEADS, HEAD_SIZE
        )
        segment_key = lax.dynamic_slice_in_dim(request_of_row, offset, rows_per_block)
        position_key = offset + jnp.arange(rows_per_block, dtype=jnp.int32)
        allowed = (segment_query[:, None] == segment_key[None, :]) & (
            position_key[None, :] <= position_query[:, None]
        )
        running_max, running_sum, accumulated = carried_block
        score = (
            jnp.einsum(
                "tgqd,sgd->gqts", query_fourfold, block_keys, preferred_element_type=jnp.float32
            )
            * score_scale
        )
        masked = jnp.where(allowed, score, negative_large)
        new_max = jnp.maximum(running_max, jnp.max(masked, axis=-1))
        weights = jnp.where(allowed, jnp.exp(masked - new_max[..., None]), 0.0)
        factor = jnp.exp(running_max - new_max)
        running_sum = running_sum * factor + jnp.sum(weights, axis=-1)
        accumulated = accumulated * factor[..., None] + jnp.einsum(
            "gqts,sgd->gqtd",
            weights.astype(jnp.bfloat16),
            block_values,
            preferred_element_type=jnp.float32,
        )
        return (new_max, running_sum, accumulated)

    running_max, running_sum, accumulated = lax.fori_loop(
        0, piece_rows // rows_per_block, one_block, start_state
    )
    context = jnp.transpose(accumulated / running_sum[..., None], (2, 0, 1, 3)).reshape(
        token_rows, QUERY_HEADS * HEAD_SIZE
    )
    mixed_rows = resid.astype(jnp.float32) + context
    mean_square = jnp.mean(mixed_rows * mixed_rows, axis=1, keepdims=True)
    normed = (mixed_rows * lax.rsqrt(mean_square + 1e-06) * norm_gain).astype(jnp.bfloat16)
    pair_expert = expert_ids.reshape(-1)
    hit_table = (pair_expert[:, None] == jnp.arange(EXPERTS, dtype=jnp.int32)[None, :]).astype(
        jnp.int32
    )
    ranks = jnp.sum((jnp.cumsum(hit_table, axis=0) - 1) * hit_table, axis=1)
    slot_of = pair_expert * CAP + ranks
    slots_all = EXPERTS * CAP
    placing = jnp.arange(slots_all, dtype=jnp.int32)[:, None] == slot_of[None, :]
    placing = jnp.any(placing.reshape(slots_all, token_rows, TOP), axis=2).astype(jnp.bfloat16)
    outgoing = jnp.dot(placing, normed, preferred_element_type=jnp.float32).astype(jnp.bfloat16)
    local_experts = expert_gate_up.shape[0]
    outgoing = outgoing.reshape(columns, local_experts * CAP, model_width)
    shared_both = jnp.dot(
        normed, shared_gate_up.reshape(model_width, -1), preferred_element_type=jnp.float32
    ).reshape(token_rows, 2, -1)
    shared_hidden = silu_mul(shared_both[:, 0], shared_both[:, 1]).astype(jnp.bfloat16)
    shared_out = jnp.dot(shared_hidden, shared_down, preferred_element_type=jnp.float32)
    at_expert = lax.all_to_all(outgoing, "head", split_axis=0, concat_axis=0, tiled=True)
    gathered = lax.all_gather(at_expert, "req", axis=0, tiled=True)
    expert_rows = gathered.reshape(-1, model_width)
    both_parts = jnp.einsum(
        "nd,kfd->nkf", expert_rows, expert_gate_up[0], preferred_element_type=jnp.float32
    )
    hidden = silu_mul(both_parts[:, 0], both_parts[:, 1]).astype(jnp.bfloat16)
    part_out = jnp.dot(hidden, expert_down[0], preferred_element_type=jnp.float32).astype(
        jnp.bfloat16
    )
    part_sum = lax.psum_scatter(part_out, "req", scatter_dimension=0, tiled=True)
    returned = lax.all_to_all(
        part_sum.reshape(columns, local_experts * CAP, model_width),
        "head",
        split_axis=0,
        concat_axis=0,
        tiled=True,
    )
    summed = returned.reshape(slots_all, model_width)
    pair_rows = jnp.take(summed, slot_of, axis=0).reshape(token_rows, TOP, model_width)
    routed = jnp.sum(pair_rows.astype(jnp.float32) * expert_weights[:, :, None], axis=1)
    return (mixed_rows + shared_out + routed).astype(jnp.bfloat16)


def solution(mesh):
    return jax.shard_map(
        body,
        mesh=mesh,
        in_specs=(
            P(("req", "head"), None),
            P(("req", "head"), None),
            P(("req", "head"), None),
            P("req"),
            P("req", "head", None),
            P(("req", "head"), None),
            P(("req", "head"), None),
            P(),
            P(),
            P(),
            P("head", None, "req", None),
            P("head", "req", None),
        ),
        out_specs=P(("req", "head"), None),
        check_vma=False,
    )
```

```python
import functools

import jax
import jax.numpy as jnp
from jax import lax
from jax.experimental import pallas as pl
from jax.experimental.pallas import tpu as pltpu
from jax.sharding import PartitionSpec as P

QUERY_HEADS = 16
KEY_VALUE_HEADS = 4
HEAD_SIZE = 128
EXPERTS = 32
TOP = 6
CAP = 14
SLOT = 16


negative_large = -1e30


def silu_mul(gate_value, upward):
    return gate_value / (1.0 + jnp.exp(-gate_value)) * upward


def attn_kernel(q_ref, kv_ref, segq_ref, segk_ref, posq_ref, posk_ref, out_ref, *, heads, kv_heads, size):
    allowed = (segq_ref[...] == segk_ref[...]) & (posk_ref[...] <= posq_ref[...])
    frac = heads // kv_heads
    width = kv_heads * size
    for g in range(kv_heads):
        keys = kv_ref[:, g * size:(g + 1) * size]
        values = kv_ref[:, width + g * size: width + (g + 1) * size]
        for j in range(frac):
            h = g * frac + j
            qh = q_ref[:, h * size:(h + 1) * size]
            score = lax.dot_general(qh, keys, (((1,), (1,)), ((), ())), preferred_element_type=jnp.float32) * (size ** -0.5)
            masked = jnp.where(allowed, score, -1e30)
            top = jnp.max(masked, axis=1, keepdims=True)
            weights = jnp.where(allowed, jnp.exp(masked - top), 0.0)
            total = jnp.sum(weights, axis=1, keepdims=True)
            ctx = jnp.dot(weights.astype(jnp.bfloat16), values, preferred_element_type=jnp.float32)
            out_ref[:, h * size:(h + 1) * size] = ctx / total

def attention(q, kv, segq, segk, posq, posk):
    rows = q.shape[0]
    vmem = pl.BlockSpec(memory_space=pltpu.VMEM)
    return pl.pallas_call(
        functools.partial(attn_kernel, heads=16, kv_heads=4, size=128),
        out_shape=jax.ShapeDtypeStruct((rows, q.shape[1]), jnp.float32),
        in_specs=[vmem] * 6, out_specs=vmem,
    )(q, kv, segq.reshape(rows, 1), segk.reshape(1, -1), posq.reshape(rows, 1), posk.reshape(1, -1))


def body(
    hidden_in,
    queries,
    keys_values,
    request_of_row,
    page_route,
    expert_ids,
    expert_weights,
    norm_gain,
    shared_gate_up,
    shared_down,
    expert_gate_up,
    expert_down,
):
    groups = lax.axis_size("req")
    columns = lax.axis_size("head")
    token_rows = hidden_in.shape[0]
    model_width = hidden_in.shape[1]
    page_rows = token_rows // groups
    group_ids = jnp.arange(groups, dtype=jnp.int32)
    page_dest = page_route.reshape(groups)
    matches = (page_dest[None, :] == group_ids[:, None]).astype(jnp.int32)
    dest_order = jnp.sum(matches * group_ids[None, :], axis=1)

    def by_dest(array_in):
        return jnp.take(array_in.reshape(groups, page_rows, array_in.shape[1]), dest_order, axis=0)

    widths = (hidden_in.shape[1], queries.shape[1], keys_values.shape[1])
    packed = jnp.concatenate((hidden_in, queries, keys_values), axis=1)
    moved = lax.all_to_all(by_dest(packed), "req", split_axis=0, concat_axis=0, tiled=True)
    moved = moved.reshape(token_rows, sum(widths))
    resid = moved[:, : widths[0]]
    rows_of_queries = moved[:, widths[0] : widths[0] + widths[1]]
    key_value_rows = moved[:, widths[0] + widths[1] :]
    query_start = lax.axis_index("head") * token_rows
    segment_query = lax.dynamic_slice_in_dim(request_of_row, query_start, token_rows)
    position_query = query_start + jnp.arange(token_rows, dtype=jnp.int32)
    kv_piece = lax.all_gather(key_value_rows, "head", axis=0, tiled=True)
    position_key = jnp.arange(kv_piece.shape[0], dtype=jnp.int32)
    context = attention(
        rows_of_queries, kv_piece, segment_query, request_of_row, position_query, position_key
    )
    mixed_rows = resid.astype(jnp.float32) + context
    mean_square = jnp.mean(mixed_rows * mixed_rows, axis=1, keepdims=True)
    normed = (mixed_rows * lax.rsqrt(mean_square + 1e-06) * norm_gain).astype(jnp.bfloat16)
    pair_expert = expert_ids.reshape(-1)
    hit_table = (pair_expert[:, None] == jnp.arange(EXPERTS, dtype=jnp.int32)[None, :]).astype(
        jnp.int32
    )
    ranks = jnp.sum((jnp.cumsum(hit_table, axis=0) - 1) * hit_table, axis=1)
    slot_of = pair_expert * SLOT + ranks
    slots_all = EXPERTS * SLOT
    placing = jnp.arange(slots_all, dtype=jnp.int32)[:, None] == slot_of[None, :]
    placing = jnp.any(placing.reshape(slots_all, token_rows, TOP), axis=2).astype(jnp.bfloat16)
    outgoing = jnp.dot(placing, normed, preferred_element_type=jnp.float32).astype(jnp.bfloat16)
    local_experts = expert_gate_up.shape[0]
    outgoing = outgoing.reshape(columns, local_experts * SLOT, model_width)
    shared_both = jnp.einsum(
        "td,dkf->tkf", normed, shared_gate_up, preferred_element_type=jnp.float32
    )
    shared_hidden = silu_mul(shared_both[:, 0], shared_both[:, 1]).astype(jnp.bfloat16)
    shared_out = jnp.dot(shared_hidden, shared_down, preferred_element_type=jnp.float32)
    at_expert = lax.all_to_all(outgoing, "head", split_axis=0, concat_axis=0, tiled=True)
    gathered = lax.all_gather(at_expert, "req", axis=0, tiled=True)
    expert_rows = gathered.reshape(-1, model_width)
    both_parts = jnp.einsum(
        "nd,kfd->nkf", expert_rows, expert_gate_up[0], preferred_element_type=jnp.float32
    )
    hidden = silu_mul(both_parts[:, 0], both_parts[:, 1]).astype(jnp.bfloat16)
    part_out = jnp.dot(hidden, expert_down[0], preferred_element_type=jnp.float32).astype(
        jnp.bfloat16
    )
    part_sum = lax.psum_scatter(part_out, "req", scatter_dimension=0, tiled=True)
    returned = lax.all_to_all(
        part_sum.reshape(columns, local_experts * SLOT, model_width),
        "head",
        split_axis=0,
        concat_axis=0,
        tiled=True,
    )
    summed = returned.reshape(slots_all, model_width)
    pair_rows = jnp.take(summed, slot_of, axis=0).reshape(token_rows, TOP, model_width)
    routed = jnp.sum(pair_rows.astype(jnp.float32) * expert_weights[:, :, None], axis=1)
    return (mixed_rows + shared_out + routed).astype(jnp.bfloat16)


def solution(mesh):
    return jax.shard_map(
        body,
        mesh=mesh,
        in_specs=(
            P(("req", "head"), None),
            P(("req", "head"), None),
            P(("req", "head"), None),
            P("req"),
            P("req", "head", None),
            P(("req", "head"), None),
            P(("req", "head"), None),
            P(),
            P(),
            P(),
            P("head", None, "req", None),
            P("head", "req", None),
        ),
        out_specs=P(("req", "head"), None),
        check_vma=False,
    )
```

```python
import functools

import jax
import jax.numpy as jnp
from jax import lax
from jax.experimental import pallas as pl
from jax.experimental.pallas import tpu as pltpu
from jax.sharding import PartitionSpec as P

QUERY_HEADS = 16
KEY_VALUE_HEADS = 4
HEAD_SIZE = 128
EXPERTS = 32
TOP = 6
CAP = 14
SLOT = 16


negative_large = -1e30


def silu_mul(gate_value, upward):
    return gate_value / (1.0 + jnp.exp(-gate_value)) * upward


def attn_kernel(q_ref, kv_ref, segq_ref, segk_ref, posq_ref, posk_ref, out_ref, *, heads, kv_heads, size):
    allowed = (segq_ref[...] == segk_ref[...]) & (posk_ref[...] <= posq_ref[...])
    frac = heads // kv_heads
    width = kv_heads * size
    for g in range(kv_heads):
        keys = kv_ref[:, g * size:(g + 1) * size]
        values = kv_ref[:, width + g * size: width + (g + 1) * size]
        for j in range(frac):
            h = g * frac + j
            qh = q_ref[:, h * size:(h + 1) * size]
            score = lax.dot_general(qh, keys, (((1,), (1,)), ((), ())), preferred_element_type=jnp.float32) * (size ** -0.5)
            masked = jnp.where(allowed, score, -1e30)
            top = jnp.max(masked, axis=1, keepdims=True)
            weights = jnp.where(allowed, jnp.exp(masked - top), 0.0)
            total = jnp.sum(weights, axis=1, keepdims=True)
            ctx = jnp.dot(weights.astype(jnp.bfloat16), values, preferred_element_type=jnp.float32)
            out_ref[:, h * size:(h + 1) * size] = ctx / total

def attention(q, kv, segq, segk, posq, posk):
    rows = q.shape[0]
    vmem = pl.BlockSpec(memory_space=pltpu.VMEM)
    return pl.pallas_call(
        functools.partial(attn_kernel, heads=16, kv_heads=4, size=128),
        out_shape=jax.ShapeDtypeStruct((rows, q.shape[1]), jnp.float32),
        in_specs=[vmem] * 6, out_specs=vmem,
    )(q, kv, segq.reshape(rows, 1), segk.reshape(1, -1), posq.reshape(rows, 1), posk.reshape(1, -1))


def body(
    hidden_in,
    queries,
    keys_values,
    request_of_row,
    page_route,
    expert_ids,
    expert_weights,
    norm_gain,
    shared_gate_up,
    shared_down,
    expert_gate_up,
    expert_down,
):
    groups = lax.axis_size("req")
    columns = lax.axis_size("head")
    token_rows = hidden_in.shape[0]
    model_width = hidden_in.shape[1]
    page_rows = token_rows // groups
    group_ids = jnp.arange(groups, dtype=jnp.int32)
    page_dest = page_route.reshape(groups)
    matches = (page_dest[None, :] == group_ids[:, None]).astype(jnp.int32)
    dest_order = jnp.sum(matches * group_ids[None, :], axis=1)

    def by_dest(array_in):
        return jnp.take(array_in.reshape(groups, page_rows, array_in.shape[1]), dest_order, axis=0)

    moved_kv = lax.all_to_all(by_dest(keys_values), "req", split_axis=0, concat_axis=0, tiled=True)
    key_value_rows = moved_kv.reshape(token_rows, keys_values.shape[1])
    kv_piece = lax.all_gather(key_value_rows, "head", axis=0, tiled=True)
    widths = (hidden_in.shape[1], queries.shape[1])
    packed = jnp.concatenate((hidden_in, queries), axis=1)
    moved = lax.all_to_all(by_dest(packed), "req", split_axis=0, concat_axis=0, tiled=True)
    moved = moved.reshape(token_rows, sum(widths))
    resid = moved[:, : widths[0]]
    rows_of_queries = moved[:, widths[0] :]
    query_start = lax.axis_index("head") * token_rows
    segment_query = lax.dynamic_slice_in_dim(request_of_row, query_start, token_rows)
    position_query = query_start + jnp.arange(token_rows, dtype=jnp.int32)
    position_key = jnp.arange(kv_piece.shape[0], dtype=jnp.int32)
    context = attention(
        rows_of_queries, kv_piece, segment_query, request_of_row, position_query, position_key
    )
    mixed_rows = resid.astype(jnp.float32) + context
    mean_square = jnp.mean(mixed_rows * mixed_rows, axis=1, keepdims=True)
    normed = (mixed_rows * lax.rsqrt(mean_square + 1e-06) * norm_gain).astype(jnp.bfloat16)
    pair_expert = expert_ids.reshape(-1)
    hit_table = (pair_expert[:, None] == jnp.arange(EXPERTS, dtype=jnp.int32)[None, :]).astype(
        jnp.int32
    )
    ranks = jnp.sum((jnp.cumsum(hit_table, axis=0) - 1) * hit_table, axis=1)
    slot_of = pair_expert * SLOT + ranks
    slots_all = EXPERTS * SLOT
    placing = jnp.arange(slots_all, dtype=jnp.int32)[:, None] == slot_of[None, :]
    placing = jnp.any(placing.reshape(slots_all, token_rows, TOP), axis=2).astype(jnp.bfloat16)
    outgoing = jnp.dot(placing, normed, preferred_element_type=jnp.float32).astype(jnp.bfloat16)
    local_experts = expert_gate_up.shape[0]
    outgoing = outgoing.reshape(columns, local_experts * SLOT, model_width)
    shared_both = jnp.einsum(
        "td,dkf->tkf", normed, shared_gate_up, preferred_element_type=jnp.float32
    )
    shared_hidden = silu_mul(shared_both[:, 0], shared_both[:, 1]).astype(jnp.bfloat16)
    shared_out = jnp.dot(shared_hidden, shared_down, preferred_element_type=jnp.float32)
    copies = jnp.broadcast_to(outgoing[None], (groups,) + outgoing.shape).reshape(
        groups * columns, local_experts * SLOT, model_width
    )
    arrived = lax.all_to_all(copies, ("req", "head"), split_axis=0, concat_axis=0, tiled=True)
    expert_rows = arrived.reshape(-1, model_width)
    both_parts = jnp.einsum(
        "nd,kfd->nkf", expert_rows, expert_gate_up[0], preferred_element_type=jnp.float32
    )
    hidden = silu_mul(both_parts[:, 0], both_parts[:, 1]).astype(jnp.bfloat16)
    part_out = jnp.dot(hidden, expert_down[0], preferred_element_type=jnp.float32).astype(
        jnp.bfloat16
    )
    returned = lax.all_to_all(
        part_out.reshape(groups * columns, local_experts * SLOT, model_width),
        ("req", "head"),
        split_axis=0,
        concat_axis=0,
        tiled=True,
    )
    returned = returned.reshape(groups, slots_all, model_width)
    pair_sum = jnp.take(returned[0], slot_of, axis=0).astype(jnp.float32)
    for part in range(1, groups):
        pair_sum = pair_sum + jnp.take(returned[part], slot_of, axis=0).astype(jnp.float32)
    pair_sum = pair_sum.reshape(token_rows, TOP, model_width)
    routed = jnp.sum(pair_sum * expert_weights[:, :, None], axis=1)
    return (mixed_rows + shared_out + routed).astype(jnp.bfloat16)


def solution(mesh):
    return jax.shard_map(
        body,
        mesh=mesh,
        in_specs=(
            P(("req", "head"), None),
            P(("req", "head"), None),
            P(("req", "head"), None),
            P("req"),
            P("req", "head", None),
            P(("req", "head"), None),
            P(("req", "head"), None),
            P(),
            P(),
            P(),
            P("head", None, "req", None),
            P("head", "req", None),
        ),
        out_specs=P(("req", "head"), None),
        check_vma=False,
    )
```

```python
import functools

import jax
import jax.numpy as jnp
from jax import lax
from jax.experimental import pallas as pl
from jax.experimental.pallas import tpu as pltpu
from jax.sharding import PartitionSpec as P

QUERY_HEADS = 16
KEY_VALUE_HEADS = 4
HEAD_SIZE = 128
EXPERTS = 32
TOP = 6
CAP = 14
SLOT = 16


negative_large = -1e30


def silu_mul(gate_value, upward):
    return gate_value / (1.0 + jnp.exp(-gate_value)) * upward


def attn_kernel(q_ref, kv_ref, segq_ref, segk_ref, posq_ref, posk_ref, out_ref, *, heads, kv_heads, size):
    allowed = (segq_ref[...] == segk_ref[...]) & (posk_ref[...] <= posq_ref[...])
    frac = heads // kv_heads
    width = kv_heads * size
    for g in range(kv_heads):
        keys = kv_ref[:, g * size:(g + 1) * size]
        values = kv_ref[:, width + g * size: width + (g + 1) * size]
        for j in range(frac):
            h = g * frac + j
            qh = q_ref[:, h * size:(h + 1) * size]
            score = lax.dot_general(qh, keys, (((1,), (1,)), ((), ())), preferred_element_type=jnp.float32) * (size ** -0.5)
            masked = jnp.where(allowed, score, -1e30)
            top = jnp.max(masked, axis=1, keepdims=True)
            weights = jnp.where(allowed, jnp.exp(masked - top), 0.0)
            total = jnp.sum(weights, axis=1, keepdims=True)
            ctx = jnp.dot(weights.astype(jnp.bfloat16), values, preferred_element_type=jnp.float32)
            out_ref[:, h * size:(h + 1) * size] = ctx / total

def attention(q, kv, segq, segk, posq, posk):
    rows = q.shape[0]
    vmem = pl.BlockSpec(memory_space=pltpu.VMEM)
    return pl.pallas_call(
        functools.partial(attn_kernel, heads=16, kv_heads=4, size=128),
        out_shape=jax.ShapeDtypeStruct((rows, q.shape[1]), jnp.float32),
        in_specs=[vmem] * 6, out_specs=vmem,
    )(q, kv, segq.reshape(rows, 1), segk.reshape(1, -1), posq.reshape(rows, 1), posk.reshape(1, -1))


def body(
    hidden_in,
    queries,
    keys_values,
    request_of_row,
    page_route,
    expert_ids,
    expert_weights,
    norm_gain,
    shared_gate_up,
    shared_down,
    expert_gate_up,
    expert_down,
):
    groups = lax.axis_size("req")
    columns = lax.axis_size("head")
    token_rows = hidden_in.shape[0]
    model_width = hidden_in.shape[1]
    page_rows = token_rows // groups
    group_ids = jnp.arange(groups, dtype=jnp.int32)
    page_dest = page_route.reshape(groups)
    matches = (page_dest[None, :] == group_ids[:, None]).astype(jnp.int32)
    dest_order = jnp.sum(matches * group_ids[None, :], axis=1)

    def by_dest(array_in):
        return jnp.take(array_in.reshape(groups, page_rows, array_in.shape[1]), dest_order, axis=0)

    moved_kv = lax.all_to_all(by_dest(keys_values), "req", split_axis=0, concat_axis=0, tiled=True)
    key_value_rows = moved_kv.reshape(token_rows, keys_values.shape[1])
    kv_piece = lax.all_gather(key_value_rows, "head", axis=0, tiled=True)
    widths = (hidden_in.shape[1], queries.shape[1])
    packed = jnp.concatenate((hidden_in, queries), axis=1)
    moved = lax.all_to_all(by_dest(packed), "req", split_axis=0, concat_axis=0, tiled=True)
    moved = moved.reshape(token_rows, sum(widths))
    resid = moved[:, : widths[0]]
    rows_of_queries = moved[:, widths[0] :]
    query_start = lax.axis_index("head") * token_rows
    segment_query = lax.dynamic_slice_in_dim(request_of_row, query_start, token_rows)
    position_query = query_start + jnp.arange(token_rows, dtype=jnp.int32)
    position_key = jnp.arange(kv_piece.shape[0], dtype=jnp.int32)
    context = attention(
        rows_of_queries, kv_piece, segment_query, request_of_row, position_query, position_key
    )
    mixed_rows = resid.astype(jnp.float32) + context
    mean_square = jnp.mean(mixed_rows * mixed_rows, axis=1, keepdims=True)
    normed = (mixed_rows * lax.rsqrt(mean_square + 1e-06) * norm_gain).astype(jnp.bfloat16)
    pair_expert = expert_ids.reshape(-1)
    hit_table = (pair_expert[:, None] == jnp.arange(EXPERTS, dtype=jnp.int32)[None, :]).astype(
        jnp.int32
    )
    ranks = jnp.sum((jnp.cumsum(hit_table, axis=0) - 1) * hit_table, axis=1)
    slot_of = pair_expert * SLOT + ranks
    slots_all = EXPERTS * SLOT
    placing = jnp.arange(slots_all, dtype=jnp.int32)[:, None] == slot_of[None, :]
    placing = jnp.any(placing.reshape(slots_all, token_rows, TOP), axis=2).astype(jnp.bfloat16)
    outgoing = jnp.dot(placing, normed, preferred_element_type=jnp.float32).astype(jnp.bfloat16)
    local_experts = expert_gate_up.shape[0]
    outgoing = outgoing.reshape(columns, local_experts * SLOT, model_width)
    shared_both = jnp.einsum(
        "td,dkf->tkf", normed, shared_gate_up, preferred_element_type=jnp.float32
    )
    shared_hidden = silu_mul(shared_both[:, 0], shared_both[:, 1]).astype(jnp.bfloat16)
    shared_out = jnp.dot(shared_hidden, shared_down, preferred_element_type=jnp.float32)
    copies = jnp.broadcast_to(outgoing[None], (groups,) + outgoing.shape).reshape(
        groups * columns, local_experts * SLOT, model_width
    )
    arrived = lax.all_to_all(copies, ("req", "head"), split_axis=0, concat_axis=0, tiled=True)
    expert_rows = arrived.reshape(-1, model_width)
    both_parts = jnp.einsum(
        "nd,kfd->nkf", expert_rows, expert_gate_up[0], preferred_element_type=jnp.float32
    )
    hidden = silu_mul(both_parts[:, 0], both_parts[:, 1]).astype(jnp.bfloat16)
    part_out = jnp.dot(hidden, expert_down[0], preferred_element_type=jnp.float32).astype(
        jnp.bfloat16
    )
    returned = lax.all_to_all(
        part_out.reshape(groups * columns, local_experts * SLOT, model_width),
        ("req", "head"),
        split_axis=0,
        concat_axis=0,
        tiled=True,
    )
    returned = returned.reshape(groups * slots_all, model_width)
    picking = slot_of[:, None] == jnp.arange(slots_all, dtype=jnp.int32)[None, :]
    picking = jnp.tile(picking, (1, groups)).astype(jnp.bfloat16)
    pair_sum = jnp.dot(picking, returned, preferred_element_type=jnp.float32)
    pair_sum = pair_sum.reshape(token_rows, TOP, model_width)
    routed = jnp.sum(pair_sum * expert_weights[:, :, None], axis=1)
    return (mixed_rows + shared_out + routed).astype(jnp.bfloat16)


def solution(mesh):
    return jax.shard_map(
        body,
        mesh=mesh,
        in_specs=(
            P(("req", "head"), None),
            P(("req", "head"), None),
            P(("req", "head"), None),
            P("req"),
            P("req", "head", None),
            P(("req", "head"), None),
            P(("req", "head"), None),
            P(),
            P(),
            P(),
            P("head", None, "req", None),
            P("head", "req", None),
        ),
        out_specs=P(("req", "head"), None),
        check_vma=False,
    )
```

```python
import functools

import jax
import jax.numpy as jnp
from jax import lax
from jax.experimental import pallas as pl
from jax.experimental.pallas import tpu as pltpu
from jax.sharding import PartitionSpec as P

QUERY_HEADS = 16
KEY_VALUE_HEADS = 4
HEAD_SIZE = 128
EXPERTS = 32
TOP = 6
CAP = 14
SLOT = 16


negative_large = -1e30


def silu_mul(gate_value, upward):
    return gate_value / (1.0 + jnp.exp(-gate_value)) * upward


def attn_kernel(q_ref, kv_ref, segq_ref, segk_ref, posq_ref, posk_ref, out_ref, *, heads, kv_heads, size):
    allowed = (segq_ref[...] == segk_ref[...]) & (posk_ref[...] <= posq_ref[...])
    frac = heads // kv_heads
    width = kv_heads * size
    for g in range(kv_heads):
        keys = kv_ref[:, g * size:(g + 1) * size]
        values = kv_ref[:, width + g * size: width + (g + 1) * size]
        for j in range(frac):
            h = g * frac + j
            qh = q_ref[:, h * size:(h + 1) * size]
            score = lax.dot_general(qh, keys, (((1,), (1,)), ((), ())), preferred_element_type=jnp.float32) * (size ** -0.5)
            masked = jnp.where(allowed, score, -1e30)
            top = jnp.max(masked, axis=1, keepdims=True)
            weights = jnp.where(allowed, jnp.exp(masked - top), 0.0)
            total = jnp.sum(weights, axis=1, keepdims=True)
            ctx = jnp.dot(weights.astype(jnp.bfloat16), values, preferred_element_type=jnp.float32)
            out_ref[:, h * size:(h + 1) * size] = ctx / total

def attention(q, kv, segq, segk, posq, posk):
    rows = q.shape[0]
    vmem = pl.BlockSpec(memory_space=pltpu.VMEM)
    return pl.pallas_call(
        functools.partial(attn_kernel, heads=16, kv_heads=4, size=128),
        out_shape=jax.ShapeDtypeStruct((rows, q.shape[1]), jnp.float32),
        in_specs=[vmem] * 6, out_specs=vmem,
    )(q, kv, segq.reshape(rows, 1), segk.reshape(1, -1), posq.reshape(rows, 1), posk.reshape(1, -1))


def body(
    hidden_in,
    queries,
    keys_values,
    request_of_row,
    page_route,
    expert_ids,
    expert_weights,
    norm_gain,
    shared_gate_up,
    shared_down,
    expert_gate_up,
    expert_down,
):
    groups = lax.axis_size("req")
    columns = lax.axis_size("head")
    token_rows = hidden_in.shape[0]
    model_width = hidden_in.shape[1]
    page_rows = token_rows // groups
    group_ids = jnp.arange(groups, dtype=jnp.int32)
    page_dest = page_route.reshape(groups)
    matches = (page_dest[None, :] == group_ids[:, None]).astype(jnp.int32)
    dest_order = jnp.sum(matches * group_ids[None, :], axis=1)

    def by_dest(array_in):
        return jnp.take(array_in.reshape(groups, page_rows, array_in.shape[1]), dest_order, axis=0)

    kv_pages = by_dest(keys_values)
    kv_copies = jnp.broadcast_to(
        kv_pages[:, None], (groups, columns) + kv_pages.shape[1:]
    ).reshape((groups * columns,) + kv_pages.shape[1:])
    kv_piece = lax.all_to_all(kv_copies, ("req", "head"), split_axis=0, concat_axis=0, tiled=True)
    kv_piece = kv_piece.reshape(-1, keys_values.shape[1])
    widths = (hidden_in.shape[1], queries.shape[1])
    packed = jnp.concatenate((hidden_in, queries), axis=1)
    moved = lax.all_to_all(by_dest(packed), "req", split_axis=0, concat_axis=0, tiled=True)
    moved = moved.reshape(token_rows, sum(widths))
    resid = moved[:, : widths[0]]
    rows_of_queries = moved[:, widths[0] :]
    query_start = lax.axis_index("head") * token_rows
    segment_query = lax.dynamic_slice_in_dim(request_of_row, query_start, token_rows)
    position_query = query_start + jnp.arange(token_rows, dtype=jnp.int32)
    position_key = (
        jnp.arange(kv_piece.shape[0], dtype=jnp.int32)
        .reshape(columns, groups, page_rows)
        .transpose(1, 0, 2)
        .reshape(-1)
    )
    segment_key = (
        request_of_row.reshape(columns, groups, page_rows).transpose(1, 0, 2).reshape(-1)
    )
    context = attention(
        rows_of_queries, kv_piece, segment_query, segment_key, position_query, position_key
    )
    mixed_rows = resid.astype(jnp.float32) + context
    mean_square = jnp.mean(mixed_rows * mixed_rows, axis=1, keepdims=True)
    normed = (mixed_rows * lax.rsqrt(mean_square + 1e-06) * norm_gain).astype(jnp.bfloat16)
    pair_expert = expert_ids.reshape(-1)
    hit_table = (pair_expert[:, None] == jnp.arange(EXPERTS, dtype=jnp.int32)[None, :]).astype(
        jnp.int32
    )
    ranks = jnp.sum((jnp.cumsum(hit_table, axis=0) - 1) * hit_table, axis=1)
    slot_of = pair_expert * SLOT + ranks
    slots_all = EXPERTS * SLOT
    placing = jnp.arange(slots_all, dtype=jnp.int32)[:, None] == slot_of[None, :]
    placing = jnp.any(placing.reshape(slots_all, token_rows, TOP), axis=2).astype(jnp.bfloat16)
    outgoing = jnp.dot(placing, normed, preferred_element_type=jnp.float32).astype(jnp.bfloat16)
    local_experts = expert_gate_up.shape[0]
    outgoing = outgoing.reshape(columns, local_experts * SLOT, model_width)
    shared_both = jnp.einsum(
        "td,dkf->tkf", normed, shared_gate_up, preferred_element_type=jnp.float32
    )
    shared_hidden = silu_mul(shared_both[:, 0], shared_both[:, 1]).astype(jnp.bfloat16)
    shared_out = jnp.dot(shared_hidden, shared_down, preferred_element_type=jnp.float32)
    copies = jnp.broadcast_to(outgoing[None], (groups,) + outgoing.shape).reshape(
        groups * columns, local_experts * SLOT, model_width
    )
    arrived = lax.all_to_all(copies, ("req", "head"), split_axis=0, concat_axis=0, tiled=True)
    expert_rows = arrived.reshape(-1, model_width)
    both_parts = jnp.einsum(
        "nd,kfd->nkf", expert_rows, expert_gate_up[0], preferred_element_type=jnp.float32
    )
    hidden = silu_mul(both_parts[:, 0], both_parts[:, 1]).astype(jnp.bfloat16)
    part_out = jnp.dot(hidden, expert_down[0], preferred_element_type=jnp.float32).astype(
        jnp.bfloat16
    )
    returned = lax.all_to_all(
        part_out.reshape(groups * columns, local_experts * SLOT, model_width),
        ("req", "head"),
        split_axis=0,
        concat_axis=0,
        tiled=True,
    )
    returned = returned.reshape(groups * slots_all, model_width)
    picking = slot_of[:, None] == jnp.arange(slots_all, dtype=jnp.int32)[None, :]
    picking = jnp.tile(picking, (1, groups)).astype(jnp.bfloat16)
    pair_sum = jnp.dot(picking, returned, preferred_element_type=jnp.float32)
    pair_sum = pair_sum.reshape(token_rows, TOP, model_width)
    routed = jnp.sum(pair_sum * expert_weights[:, :, None], axis=1)
    return (mixed_rows + shared_out + routed).astype(jnp.bfloat16)


def solution(mesh):
    return jax.shard_map(
        body,
        mesh=mesh,
        in_specs=(
            P(("req", "head"), None),
            P(("req", "head"), None),
            P(("req", "head"), None),
            P("req"),
            P("req", "head", None),
            P(("req", "head"), None),
            P(("req", "head"), None),
            P(),
            P(),
            P(),
            P("head", None, "req", None),
            P("head", "req", None),
        ),
        out_specs=P(("req", "head"), None),
        check_vma=False,
    )
```

```python
import functools

import jax
import jax.numpy as jnp
from jax import lax
from jax.experimental import pallas as pl
from jax.experimental.pallas import tpu as pltpu
from jax.sharding import PartitionSpec as P


EXPERTS = 32
TOP = 6
SLOT = 16


def silu_mul(gate_value, upward):
    return gate_value / (1.0 + jnp.exp(-gate_value)) * upward


def attn_kernel(q_ref, kv_ref, segq_ref, segk_ref, posq_ref, posk_ref, out_ref, *, heads, kv_heads, size):
    allowed = (segq_ref[...] == segk_ref[...]) & (posk_ref[...] <= posq_ref[...])
    frac = heads // kv_heads
    width = kv_heads * size
    for g in range(kv_heads):
        keys = kv_ref[:, g * size:(g + 1) * size]
        values = kv_ref[:, width + g * size: width + (g + 1) * size]
        for j in range(frac):
            h = g * frac + j
            qh = q_ref[:, h * size:(h + 1) * size]
            score = lax.dot_general(qh, keys, (((1,), (1,)), ((), ())), preferred_element_type=jnp.float32) * (size ** -0.5)
            masked = jnp.where(allowed, score, -1e30)
            top = jnp.max(masked, axis=1, keepdims=True)
            weights = jnp.where(allowed, jnp.exp(masked - top), 0.0)
            total = jnp.sum(weights, axis=1, keepdims=True)
            ctx = jnp.dot(weights.astype(jnp.bfloat16), values, preferred_element_type=jnp.float32)
            out_ref[:, h * size:(h + 1) * size] = ctx / total


def attention(q, kv, segq, segk, posq, posk):
    rows = q.shape[0]
    vmem = pl.BlockSpec(memory_space=pltpu.VMEM)
    return pl.pallas_call(
        functools.partial(attn_kernel, heads=16, kv_heads=4, size=128),
        out_shape=jax.ShapeDtypeStruct((rows, q.shape[1]), jnp.float32),
        in_specs=[vmem] * 6, out_specs=vmem,
    )(q, kv, segq.reshape(rows, 1), segk.reshape(1, -1), posq.reshape(rows, 1), posk.reshape(1, -1))


def layer(
    hidden_in,
    queries,
    keys_values,
    request_of_row,
    page_route,
    expert_ids,
    expert_weights,
    norm_gain,
    shared_gate_up,
    shared_down,
    expert_gate_up,
    expert_down,
):
    groups = lax.axis_size("req")
    columns = lax.axis_size("head")
    token_rows = hidden_in.shape[0]
    model_width = hidden_in.shape[1]
    page_rows = token_rows // groups
    group_ids = jnp.arange(groups, dtype=jnp.int32)
    page_dest = page_route.reshape(groups)
    matches = (page_dest[None, :] == group_ids[:, None]).astype(jnp.int32)
    dest_order = jnp.sum(matches * group_ids[None, :], axis=1)

    down_parts = [expert_down[0]]
    for shift in range(1, groups):
        down_parts.append(
            lax.ppermute(expert_down[0], "req", [(i, (i + shift) % groups) for i in range(groups)])
        )

    def by_dest(array_in):
        return jnp.take(array_in.reshape(groups, page_rows, array_in.shape[1]), dest_order, axis=0)

    moved_kv = lax.all_to_all(by_dest(keys_values), "req", split_axis=0, concat_axis=0, tiled=True)
    key_value_rows = moved_kv.reshape(token_rows, keys_values.shape[1])
    kv_piece = lax.all_gather(key_value_rows, "head", axis=0, tiled=True)
    widths = (hidden_in.shape[1], queries.shape[1])
    packed = jnp.concatenate((hidden_in, queries), axis=1)
    moved = lax.all_to_all(by_dest(packed), "req", split_axis=0, concat_axis=0, tiled=True)
    moved = moved.reshape(token_rows, sum(widths))
    resid = moved[:, : widths[0]]
    rows_of_queries = moved[:, widths[0] :]
    query_start = lax.axis_index("head") * token_rows
    segment_query = lax.dynamic_slice_in_dim(request_of_row, query_start, token_rows)
    position_query = query_start + jnp.arange(token_rows, dtype=jnp.int32)
    position_key = jnp.arange(kv_piece.shape[0], dtype=jnp.int32)
    context = attention(
        rows_of_queries, kv_piece, segment_query, request_of_row, position_query, position_key
    )
    mixed_rows = resid.astype(jnp.float32) + context
    mean_square = jnp.mean(mixed_rows * mixed_rows, axis=1, keepdims=True)
    normed = (mixed_rows * lax.rsqrt(mean_square + 1e-06) * norm_gain).astype(jnp.bfloat16)
    pair_expert = expert_ids.reshape(-1)
    hit_table = (pair_expert[:, None] == jnp.arange(EXPERTS, dtype=jnp.int32)[None, :]).astype(
        jnp.int32
    )
    ranks = jnp.sum((jnp.cumsum(hit_table, axis=0) - 1) * hit_table, axis=1)
    slot_of = pair_expert * SLOT + ranks
    slots_all = EXPERTS * SLOT
    placing = jnp.arange(slots_all, dtype=jnp.int32)[:, None] == slot_of[None, :]
    placing = jnp.any(placing.reshape(slots_all, token_rows, TOP), axis=2).astype(jnp.bfloat16)
    outgoing = jnp.dot(placing, normed, preferred_element_type=jnp.float32).astype(jnp.bfloat16)
    local_experts = expert_gate_up.shape[0]
    outgoing = outgoing.reshape(columns, local_experts * SLOT, model_width)
    shared_both = jnp.einsum(
        "td,dkf->tkf", normed, shared_gate_up, preferred_element_type=jnp.float32
    )
    shared_hidden = silu_mul(shared_both[:, 0], shared_both[:, 1]).astype(jnp.bfloat16)
    shared_out = jnp.dot(shared_hidden, shared_down, preferred_element_type=jnp.float32)
    copies = jnp.broadcast_to(outgoing[None], (groups,) + outgoing.shape).reshape(
        groups * columns, local_experts * SLOT, model_width
    )
    arrived = lax.all_to_all(copies, ("req", "head"), split_axis=0, concat_axis=0, tiled=True)
    expert_rows = arrived.reshape(-1, model_width)
    both_parts = jnp.einsum(
        "nd,kfd->nkf", expert_rows, expert_gate_up[0], preferred_element_type=jnp.float32
    )
    hidden = silu_mul(both_parts[:, 0], both_parts[:, 1]).astype(jnp.bfloat16)
    hidden = hidden.reshape(groups, columns * local_experts * SLOT, hidden.shape[-1])
    hidden_parts = lax.all_to_all(hidden, "req", split_axis=0, concat_axis=0, tiled=True)
    out_rows = None
    for shift in range(groups):
        part_index = (lax.axis_index("req") - shift) % groups
        hidden_part = lax.dynamic_index_in_dim(hidden_parts, part_index, 0, keepdims=False)
        product = jnp.dot(hidden_part, down_parts[shift], preferred_element_type=jnp.float32)
        out_rows = product if out_rows is None else out_rows + product
    returned = lax.all_to_all(
        out_rows.astype(jnp.bfloat16).reshape(columns, local_experts * SLOT, model_width),
        "head",
        split_axis=0,
        concat_axis=0,
        tiled=True,
    )
    returned = returned.reshape(slots_all, model_width)
    picking = (slot_of[:, None] == jnp.arange(slots_all, dtype=jnp.int32)[None, :]).astype(
        jnp.bfloat16
    )
    pair_sum = jnp.dot(picking, returned, preferred_element_type=jnp.float32)
    pair_sum = pair_sum.reshape(token_rows, TOP, model_width)
    routed = jnp.sum(pair_sum * expert_weights[:, :, None], axis=1)
    return (mixed_rows + shared_out + routed).astype(jnp.bfloat16)


def solution(mesh):
    return jax.shard_map(
        layer,
        mesh=mesh,
        in_specs=(
            P(("req", "head"), None),
            P(("req", "head"), None),
            P(("req", "head"), None),
            P("req"),
            P("req", "head", None),
            P(("req", "head"), None),
            P(("req", "head"), None),
            P(),
            P(),
            P(),
            P("head", None, "req", None),
            P("head", "req", None),
        ),
        out_specs=P(("req", "head"), None),
        check_vma=False,
    )
```

```python
import functools

import jax
import jax.numpy as jnp
from jax import lax
from jax.experimental import pallas as pl
from jax.experimental.pallas import tpu as pltpu
from jax.sharding import PartitionSpec as P


EXPERTS = 32
TOP = 6
SLOT = 16


def silu_mul(gate_value, upward):
    return gate_value / (1.0 + jnp.exp(-gate_value)) * upward


def attn_kernel(q_ref, kv_ref, segq_ref, segk_ref, posq_ref, posk_ref, out_ref, *, heads, kv_heads, size):
    allowed = (segq_ref[...] == segk_ref[...]) & (posk_ref[...] <= posq_ref[...])
    frac = heads // kv_heads
    width = kv_heads * size
    for g in range(kv_heads):
        keys = kv_ref[:, g * size:(g + 1) * size]
        values = kv_ref[:, width + g * size: width + (g + 1) * size]
        for j in range(frac):
            h = g * frac + j
            qh = q_ref[:, h * size:(h + 1) * size]
            score = lax.dot_general(qh, keys, (((1,), (1,)), ((), ())), preferred_element_type=jnp.float32) * (size ** -0.5)
            masked = jnp.where(allowed, score, -1e30)
            top = jnp.max(masked, axis=1, keepdims=True)
            weights = jnp.where(allowed, jnp.exp(masked - top), 0.0)
            total = jnp.sum(weights, axis=1, keepdims=True)
            ctx = jnp.dot(weights.astype(jnp.bfloat16), values, preferred_element_type=jnp.float32)
            out_ref[:, h * size:(h + 1) * size] = ctx / total


def attention(q, kv, segq, segk, posq, posk):
    rows = q.shape[0]
    vmem = pl.BlockSpec(memory_space=pltpu.VMEM)
    return pl.pallas_call(
        functools.partial(attn_kernel, heads=16, kv_heads=4, size=128),
        out_shape=jax.ShapeDtypeStruct((rows, q.shape[1]), jnp.float32),
        in_specs=[vmem] * 6, out_specs=vmem,
    )(q, kv, segq.reshape(rows, 1), segk.reshape(1, -1), posq.reshape(rows, 1), posk.reshape(1, -1))


def layer(
    hidden_in,
    queries,
    keys_values,
    request_of_row,
    page_route,
    expert_ids,
    expert_weights,
    norm_gain,
    shared_gate_up,
    shared_down,
    expert_gate_up,
    expert_down,
):
    groups = lax.axis_size("req")
    columns = lax.axis_size("head")
    token_rows = hidden_in.shape[0]
    model_width = hidden_in.shape[1]
    page_rows = token_rows // groups
    group_ids = jnp.arange(groups, dtype=jnp.int32)
    page_dest = page_route.reshape(groups)
    matches = (page_dest[None, :] == group_ids[:, None]).astype(jnp.int32)
    dest_order = jnp.sum(matches * group_ids[None, :], axis=1)

    def by_dest(array_in):
        return jnp.take(array_in.reshape(groups, page_rows, array_in.shape[1]), dest_order, axis=0)

    moved_kv = lax.all_to_all(by_dest(keys_values), "req", split_axis=0, concat_axis=0, tiled=True)
    key_value_rows = moved_kv.reshape(token_rows, keys_values.shape[1])
    kv_piece = lax.all_gather(key_value_rows, "head", axis=0, tiled=True)
    widths = (hidden_in.shape[1], queries.shape[1])
    packed = jnp.concatenate((hidden_in, queries), axis=1)
    moved = lax.all_to_all(by_dest(packed), "req", split_axis=0, concat_axis=0, tiled=True)
    down_own, moved = lax.optimization_barrier((expert_down[0], moved))
    down_parts = [down_own]
    for shift in range(1, groups):
        down_parts.append(
            lax.ppermute(
                down_own, "req", [(i, (i + shift) % groups) for i in range(groups)]
            )
        )

    moved = moved.reshape(token_rows, sum(widths))
    resid = moved[:, : widths[0]]
    rows_of_queries = moved[:, widths[0] :]
    query_start = lax.axis_index("head") * token_rows
    segment_query = lax.dynamic_slice_in_dim(request_of_row, query_start, token_rows)
    position_query = query_start + jnp.arange(token_rows, dtype=jnp.int32)
    position_key = jnp.arange(kv_piece.shape[0], dtype=jnp.int32)
    context = attention(
        rows_of_queries, kv_piece, segment_query, request_of_row, position_query, position_key
    )
    mixed_rows = resid.astype(jnp.float32) + context
    mean_square = jnp.mean(mixed_rows * mixed_rows, axis=1, keepdims=True)
    normed = (mixed_rows * lax.rsqrt(mean_square + 1e-06) * norm_gain).astype(jnp.bfloat16)
    pair_expert = expert_ids.reshape(-1)
    hit_table = (pair_expert[:, None] == jnp.arange(EXPERTS, dtype=jnp.int32)[None, :]).astype(
        jnp.int32
    )
    ranks = jnp.sum((jnp.cumsum(hit_table, axis=0) - 1) * hit_table, axis=1)
    slot_of = pair_expert * SLOT + ranks
    slots_all = EXPERTS * SLOT
    placing = jnp.arange(slots_all, dtype=jnp.int32)[:, None] == slot_of[None, :]
    placing = jnp.any(placing.reshape(slots_all, token_rows, TOP), axis=2).astype(jnp.bfloat16)
    outgoing = jnp.dot(placing, normed, preferred_element_type=jnp.float32).astype(jnp.bfloat16)
    local_experts = expert_gate_up.shape[0]
    outgoing = outgoing.reshape(columns, local_experts * SLOT, model_width)
    shared_both = jnp.einsum(
        "td,dkf->tkf", normed, shared_gate_up, preferred_element_type=jnp.float32
    )
    shared_hidden = silu_mul(shared_both[:, 0], shared_both[:, 1]).astype(jnp.bfloat16)
    shared_out = jnp.dot(shared_hidden, shared_down, preferred_element_type=jnp.float32)
    copies = jnp.broadcast_to(outgoing[None], (groups,) + outgoing.shape).reshape(
        groups * columns, local_experts * SLOT, model_width
    )
    arrived = lax.all_to_all(copies, ("req", "head"), split_axis=0, concat_axis=0, tiled=True)
    expert_rows = arrived.reshape(-1, model_width)
    both_parts = jnp.einsum(
        "nd,kfd->nkf", expert_rows, expert_gate_up[0], preferred_element_type=jnp.float32
    )
    hidden = silu_mul(both_parts[:, 0], both_parts[:, 1]).astype(jnp.bfloat16)
    hidden = hidden.reshape(groups, columns * local_experts * SLOT, hidden.shape[-1])
    hidden_parts = lax.all_to_all(hidden, "req", split_axis=0, concat_axis=0, tiled=True)
    out_rows = None
    for shift in range(groups):
        part_index = (lax.axis_index("req") - shift) % groups
        hidden_part = lax.dynamic_index_in_dim(hidden_parts, part_index, 0, keepdims=False)
        product = jnp.dot(hidden_part, down_parts[shift], preferred_element_type=jnp.float32)
        out_rows = product if out_rows is None else out_rows + product
    returned = lax.all_to_all(
        out_rows.astype(jnp.bfloat16).reshape(columns, local_experts * SLOT, model_width),
        "head",
        split_axis=0,
        concat_axis=0,
        tiled=True,
    )
    returned = returned.reshape(slots_all, model_width)
    picking = (slot_of[:, None] == jnp.arange(slots_all, dtype=jnp.int32)[None, :]).astype(
        jnp.bfloat16
    )
    pair_sum = jnp.dot(picking, returned, preferred_element_type=jnp.float32)
    pair_sum = pair_sum.reshape(token_rows, TOP, model_width)
    routed = jnp.sum(pair_sum * expert_weights[:, :, None], axis=1)
    return (mixed_rows + shared_out + routed).astype(jnp.bfloat16)


def solution(mesh):
    return jax.shard_map(
        layer,
        mesh=mesh,
        in_specs=(
            P(("req", "head"), None),
            P(("req", "head"), None),
            P(("req", "head"), None),
            P("req"),
            P("req", "head", None),
            P(("req", "head"), None),
            P(("req", "head"), None),
            P(),
            P(),
            P(),
            P("head", None, "req", None),
            P("head", "req", None),
        ),
        out_specs=P(("req", "head"), None),
        check_vma=False,
    )
```

```python
import functools

import jax
import jax.numpy as jnp
from jax import lax
from jax.experimental import pallas as pl
from jax.experimental.pallas import tpu as pltpu
from jax.sharding import PartitionSpec as P


EXPERTS = 32
TOP = 6
SLOT = 16


def silu_mul(gate_value, upward):
    return gate_value / (1.0 + jnp.exp(-gate_value)) * upward


def attn_kernel(q_ref, kv_ref, segq_ref, segk_ref, posq_ref, posk_ref, out_ref, *, heads, kv_heads, size):
    allowed = (segq_ref[...] == segk_ref[...]) & (posk_ref[...] <= posq_ref[...])
    frac = heads // kv_heads
    width = kv_heads * size
    for g in range(kv_heads):
        keys = kv_ref[:, g * size:(g + 1) * size]
        values = kv_ref[:, width + g * size: width + (g + 1) * size]
        for j in range(frac):
            h = g * frac + j
            qh = q_ref[:, h * size:(h + 1) * size]
            score = lax.dot_general(qh, keys, (((1,), (1,)), ((), ())), preferred_element_type=jnp.float32) * (size ** -0.5)
            masked = jnp.where(allowed, score, -1e30)
            top = jnp.max(masked, axis=1, keepdims=True)
            weights = jnp.where(allowed, jnp.exp(masked - top), 0.0)
            total = jnp.sum(weights, axis=1, keepdims=True)
            ctx = jnp.dot(weights.astype(jnp.bfloat16), values, preferred_element_type=jnp.float32)
            out_ref[:, h * size:(h + 1) * size] = ctx / total


def attention(q, kv, segq, segk, posq, posk):
    rows = q.shape[0]
    vmem = pl.BlockSpec(memory_space=pltpu.VMEM)
    return pl.pallas_call(
        functools.partial(attn_kernel, heads=16, kv_heads=4, size=128),
        out_shape=jax.ShapeDtypeStruct((rows, q.shape[1]), jnp.float32),
        in_specs=[vmem] * 6, out_specs=vmem,
    )(q, kv, segq.reshape(rows, 1), segk.reshape(1, -1), posq.reshape(rows, 1), posk.reshape(1, -1))


def layer(
    hidden_in,
    queries,
    keys_values,
    request_of_row,
    page_route,
    expert_ids,
    expert_weights,
    norm_gain,
    shared_gate_up,
    shared_down,
    expert_gate_up,
    expert_down,
):
    groups = lax.axis_size("req")
    columns = lax.axis_size("head")
    token_rows = hidden_in.shape[0]
    model_width = hidden_in.shape[1]
    page_rows = token_rows // groups
    group_ids = jnp.arange(groups, dtype=jnp.int32)
    page_dest = page_route.reshape(groups)
    matches = (page_dest[None, :] == group_ids[:, None]).astype(jnp.int32)
    dest_order = jnp.sum(matches * group_ids[None, :], axis=1)

    def by_dest(array_in):
        return jnp.take(array_in.reshape(groups, page_rows, array_in.shape[1]), dest_order, axis=0)

    moved_kv = lax.all_to_all(by_dest(keys_values), "req", split_axis=0, concat_axis=0, tiled=True)
    key_value_rows = moved_kv.reshape(token_rows, keys_values.shape[1])
    kv_piece = lax.all_gather(key_value_rows, "head", axis=0, tiled=True)
    widths = (hidden_in.shape[1], queries.shape[1])
    packed = jnp.concatenate((hidden_in, queries), axis=1)
    moved = lax.all_to_all(by_dest(packed), "req", split_axis=0, concat_axis=0, tiled=True)
    gate_own, down_own, moved = lax.optimization_barrier(
        (expert_gate_up[0], expert_down[0], moved)
    )
    gate_parts, down_parts = [gate_own], [down_own]
    for shift in range(1, groups):
        ring = [(i, (i + shift) % groups) for i in range(groups)]
        gate_parts.append(lax.ppermute(gate_own, "req", ring))
        down_parts.append(lax.ppermute(down_own, "req", ring))
    moved = moved.reshape(token_rows, sum(widths))
    resid = moved[:, : widths[0]]
    rows_of_queries = moved[:, widths[0] :]
    query_start = lax.axis_index("head") * token_rows
    segment_query = lax.dynamic_slice_in_dim(request_of_row, query_start, token_rows)
    position_query = query_start + jnp.arange(token_rows, dtype=jnp.int32)
    position_key = jnp.arange(kv_piece.shape[0], dtype=jnp.int32)
    context = attention(
        rows_of_queries, kv_piece, segment_query, request_of_row, position_query, position_key
    )
    mixed_rows = resid.astype(jnp.float32) + context
    mean_square = jnp.mean(mixed_rows * mixed_rows, axis=1, keepdims=True)
    normed = (mixed_rows * lax.rsqrt(mean_square + 1e-06) * norm_gain).astype(jnp.bfloat16)
    pair_expert = expert_ids.reshape(-1)
    hit_table = (pair_expert[:, None] == jnp.arange(EXPERTS, dtype=jnp.int32)[None, :]).astype(
        jnp.int32
    )
    ranks = jnp.sum((jnp.cumsum(hit_table, axis=0) - 1) * hit_table, axis=1)
    slot_of = pair_expert * SLOT + ranks
    slots_all = EXPERTS * SLOT
    placing = jnp.arange(slots_all, dtype=jnp.int32)[:, None] == slot_of[None, :]
    placing = jnp.any(placing.reshape(slots_all, token_rows, TOP), axis=2).astype(jnp.bfloat16)
    outgoing = jnp.dot(placing, normed, preferred_element_type=jnp.float32).astype(jnp.bfloat16)
    local_experts = expert_gate_up.shape[0]
    outgoing = outgoing.reshape(columns, local_experts * SLOT, model_width)
    shared_both = jnp.einsum(
        "td,dkf->tkf", normed, shared_gate_up, preferred_element_type=jnp.float32
    )
    shared_hidden = silu_mul(shared_both[:, 0], shared_both[:, 1]).astype(jnp.bfloat16)
    shared_out = jnp.dot(shared_hidden, shared_down, preferred_element_type=jnp.float32)
    arrived = lax.all_to_all(outgoing, "head", split_axis=0, concat_axis=0, tiled=True)
    expert_rows = arrived.reshape(-1, model_width)
    out_rows = None
    for shift in range(groups):
        gate_value = jnp.dot(
            expert_rows, gate_parts[shift][0].T, preferred_element_type=jnp.float32
        )
        upward = jnp.dot(expert_rows, gate_parts[shift][1].T, preferred_element_type=jnp.float32)
        hidden_part = silu_mul(gate_value, upward).astype(jnp.bfloat16)
        product = jnp.dot(hidden_part, down_parts[shift], preferred_element_type=jnp.float32)
        out_rows = product if out_rows is None else out_rows + product
    returned = lax.all_to_all(
        out_rows.astype(jnp.bfloat16).reshape(columns, local_experts * SLOT, model_width),
        "head",
        split_axis=0,
        concat_axis=0,
        tiled=True,
    )
    returned = returned.reshape(slots_all, model_width)
    picking = (slot_of[:, None] == jnp.arange(slots_all, dtype=jnp.int32)[None, :]).astype(
        jnp.bfloat16
    )
    pair_sum = jnp.dot(picking, returned, preferred_element_type=jnp.float32)
    pair_sum = pair_sum.reshape(token_rows, TOP, model_width)
    routed = jnp.sum(pair_sum * expert_weights[:, :, None], axis=1)
    return (mixed_rows + shared_out + routed).astype(jnp.bfloat16)


def solution(mesh):
    return jax.shard_map(
        layer,
        mesh=mesh,
        in_specs=(
            P(("req", "head"), None),
            P(("req", "head"), None),
            P(("req", "head"), None),
            P("req"),
            P("req", "head", None),
            P(("req", "head"), None),
            P(("req", "head"), None),
            P(),
            P(),
            P(),
            P("head", None, "req", None),
            P("head", "req", None),
        ),
        out_specs=P(("req", "head"), None),
        check_vma=False,
    )
```

```python
import functools

import jax
import jax.numpy as jnp
from jax import lax
from jax.experimental import pallas as pl
from jax.experimental.pallas import tpu as pltpu
from jax.sharding import PartitionSpec as P


EXPERTS = 32
TOP = 6
SLOT = 16


def silu_mul(gate_value, upward):
    return gate_value / (1.0 + jnp.exp(-gate_value)) * upward


def attn_kernel(q_ref, kv_ref, segq_ref, segk_ref, posq_ref, posk_ref, out_ref, *, heads, kv_heads, size):
    allowed = (segq_ref[...] == segk_ref[...]) & (posk_ref[...] <= posq_ref[...])
    frac = heads // kv_heads
    width = kv_heads * size
    for g in range(kv_heads):
        keys = kv_ref[:, g * size:(g + 1) * size]
        values = kv_ref[:, width + g * size: width + (g + 1) * size]
        for j in range(frac):
            h = g * frac + j
            qh = q_ref[:, h * size:(h + 1) * size]
            score = lax.dot_general(qh, keys, (((1,), (1,)), ((), ())), preferred_element_type=jnp.float32) * (size ** -0.5)
            masked = jnp.where(allowed, score, -1e30)
            top = jnp.max(masked, axis=1, keepdims=True)
            weights = jnp.where(allowed, jnp.exp(masked - top), 0.0)
            total = jnp.sum(weights, axis=1, keepdims=True)
            ctx = jnp.dot(weights.astype(jnp.bfloat16), values, preferred_element_type=jnp.float32)
            out_ref[:, h * size:(h + 1) * size] = ctx / total


def attention(q, kv, segq, segk, posq, posk):
    rows = q.shape[0]
    vmem = pl.BlockSpec(memory_space=pltpu.VMEM)
    return pl.pallas_call(
        functools.partial(attn_kernel, heads=16, kv_heads=4, size=128),
        out_shape=jax.ShapeDtypeStruct((rows, q.shape[1]), jnp.float32),
        in_specs=[vmem] * 6, out_specs=vmem,
    )(q, kv, segq.reshape(rows, 1), segk.reshape(1, -1), posq.reshape(rows, 1), posk.reshape(1, -1))


def layer(
    hidden_in,
    queries,
    keys_values,
    request_of_row,
    page_route,
    expert_ids,
    expert_weights,
    norm_gain,
    shared_gate_up,
    shared_down,
    expert_gate_up,
    expert_down,
):
    groups = lax.axis_size("req")
    columns = lax.axis_size("head")
    token_rows = hidden_in.shape[0]
    model_width = hidden_in.shape[1]
    page_rows = token_rows // groups
    group_ids = jnp.arange(groups, dtype=jnp.int32)
    page_dest = page_route.reshape(groups)
    matches = (page_dest[None, :] == group_ids[:, None]).astype(jnp.int32)
    dest_order = jnp.sum(matches * group_ids[None, :], axis=1)

    def by_dest(array_in):
        return jnp.take(array_in.reshape(groups, page_rows, array_in.shape[1]), dest_order, axis=0)

    moved_kv = lax.all_to_all(by_dest(keys_values), "req", split_axis=0, concat_axis=0, tiled=True)
    key_value_rows = moved_kv.reshape(token_rows, keys_values.shape[1])
    kv_piece = lax.all_gather(key_value_rows, "head", axis=0, tiled=True)
    widths = (hidden_in.shape[1], queries.shape[1])
    packed = jnp.concatenate((hidden_in, queries), axis=1)
    moved = lax.all_to_all(by_dest(packed), "req", split_axis=0, concat_axis=0, tiled=True)
    gate_own, down_own, moved = lax.optimization_barrier(
        (expert_gate_up[0], expert_down[0], moved)
    )
    upward_ring = [(i, (i + 1) % groups) for i in range(groups)]
    downward_ring = [(i, (i - 1) % groups) for i in range(groups)]
    half = gate_own.shape[1] // 2
    gate_below = lax.ppermute(gate_own, "req", upward_ring)
    down_below = lax.ppermute(down_own, "req", upward_ring)
    gate_above = lax.ppermute(gate_own, "req", downward_ring)
    down_above = lax.ppermute(down_own, "req", downward_ring)
    gate_far_low = lax.ppermute(gate_below[:, :half], "req", upward_ring)
    down_far_low = lax.ppermute(down_below[:half], "req", upward_ring)
    gate_far_high = lax.ppermute(gate_above[:, half:], "req", downward_ring)
    down_far_high = lax.ppermute(down_above[half:], "req", downward_ring)
    weight_sets = (
        (gate_own, down_own),
        (gate_below, down_below),
        (gate_above, down_above),
        (gate_far_low, down_far_low),
        (gate_far_high, down_far_high),
    )
    moved = moved.reshape(token_rows, sum(widths))
    resid = moved[:, : widths[0]]
    rows_of_queries = moved[:, widths[0] :]
    query_start = lax.axis_index("head") * token_rows
    segment_query = lax.dynamic_slice_in_dim(request_of_row, query_start, token_rows)
    position_query = query_start + jnp.arange(token_rows, dtype=jnp.int32)
    position_key = jnp.arange(kv_piece.shape[0], dtype=jnp.int32)
    context = attention(
        rows_of_queries, kv_piece, segment_query, request_of_row, position_query, position_key
    )
    mixed_rows = resid.astype(jnp.float32) + context
    mean_square = jnp.mean(mixed_rows * mixed_rows, axis=1, keepdims=True)
    normed = (mixed_rows * lax.rsqrt(mean_square + 1e-06) * norm_gain).astype(jnp.bfloat16)
    pair_expert = expert_ids.reshape(-1)
    hit_table = (pair_expert[:, None] == jnp.arange(EXPERTS, dtype=jnp.int32)[None, :]).astype(
        jnp.int32
    )
    ranks = jnp.sum((jnp.cumsum(hit_table, axis=0) - 1) * hit_table, axis=1)
    slot_of = pair_expert * SLOT + ranks
    slots_all = EXPERTS * SLOT
    placing = jnp.arange(slots_all, dtype=jnp.int32)[:, None] == slot_of[None, :]
    placing = jnp.any(placing.reshape(slots_all, token_rows, TOP), axis=2).astype(jnp.bfloat16)
    outgoing = jnp.dot(placing, normed, preferred_element_type=jnp.float32).astype(jnp.bfloat16)
    local_experts = expert_gate_up.shape[0]
    outgoing = outgoing.reshape(columns, local_experts * SLOT, model_width)
    shared_both = jnp.einsum(
        "td,dkf->tkf", normed, shared_gate_up, preferred_element_type=jnp.float32
    )
    shared_hidden = silu_mul(shared_both[:, 0], shared_both[:, 1]).astype(jnp.bfloat16)
    shared_out = jnp.dot(shared_hidden, shared_down, preferred_element_type=jnp.float32)
    arrived = lax.all_to_all(outgoing, "head", split_axis=0, concat_axis=0, tiled=True)
    expert_rows = arrived.reshape(-1, model_width)
    out_rows = None
    for gate_weights, down_weights in weight_sets:
        gate_value = jnp.dot(expert_rows, gate_weights[0].T, preferred_element_type=jnp.float32)
        upward = jnp.dot(expert_rows, gate_weights[1].T, preferred_element_type=jnp.float32)
        hidden_part = silu_mul(gate_value, upward).astype(jnp.bfloat16)
        product = jnp.dot(hidden_part, down_weights, preferred_element_type=jnp.float32)
        out_rows = product if out_rows is None else out_rows + product
    returned = lax.all_to_all(
        out_rows.astype(jnp.bfloat16).reshape(columns, local_experts * SLOT, model_width),
        "head",
        split_axis=0,
        concat_axis=0,
        tiled=True,
    )
    returned = returned.reshape(slots_all, model_width)
    picking = (slot_of[:, None] == jnp.arange(slots_all, dtype=jnp.int32)[None, :]).astype(
        jnp.bfloat16
    )
    pair_sum = jnp.dot(picking, returned, preferred_element_type=jnp.float32)
    pair_sum = pair_sum.reshape(token_rows, TOP, model_width)
    routed = jnp.sum(pair_sum * expert_weights[:, :, None], axis=1)
    return (mixed_rows + shared_out + routed).astype(jnp.bfloat16)


def solution(mesh):
    return jax.shard_map(
        layer,
        mesh=mesh,
        in_specs=(
            P(("req", "head"), None),
            P(("req", "head"), None),
            P(("req", "head"), None),
            P("req"),
            P("req", "head", None),
            P(("req", "head"), None),
            P(("req", "head"), None),
            P(),
            P(),
            P(),
            P("head", None, "req", None),
            P("head", "req", None),
        ),
        out_specs=P(("req", "head"), None),
        check_vma=False,
    )
```

```python
import functools

import jax
import jax.numpy as jnp
from jax import lax
from jax.experimental import pallas as pl
from jax.experimental.pallas import tpu as pltpu
from jax.sharding import PartitionSpec as P


EXPERTS = 32
TOP = 6
SLOT = 16


def silu_mul(gate_value, upward):
    return gate_value / (1.0 + jnp.exp(-gate_value)) * upward


def attn_kernel(q_ref, kv_ref, segq_ref, segk_ref, posq_ref, posk_ref, out_ref, *, heads, kv_heads, size):
    allowed = (segq_ref[...] == segk_ref[...]) & (posk_ref[...] <= posq_ref[...])
    frac = heads // kv_heads
    width = kv_heads * size
    for g in range(kv_heads):
        keys = kv_ref[:, g * size:(g + 1) * size]
        values = kv_ref[:, width + g * size: width + (g + 1) * size]
        for j in range(frac):
            h = g * frac + j
            qh = q_ref[:, h * size:(h + 1) * size]
            score = lax.dot_general(qh, keys, (((1,), (1,)), ((), ())), preferred_element_type=jnp.float32) * (size ** -0.5)
            masked = jnp.where(allowed, score, -1e30)
            top = jnp.max(masked, axis=1, keepdims=True)
            weights = jnp.where(allowed, jnp.exp(masked - top), 0.0)
            total = jnp.sum(weights, axis=1, keepdims=True)
            ctx = jnp.dot(weights.astype(jnp.bfloat16), values, preferred_element_type=jnp.float32)
            out_ref[:, h * size:(h + 1) * size] = ctx / total


def attention(q, kv, segq, segk, posq, posk):
    rows = q.shape[0]
    vmem = pl.BlockSpec(memory_space=pltpu.VMEM)
    return pl.pallas_call(
        functools.partial(attn_kernel, heads=16, kv_heads=4, size=128),
        out_shape=jax.ShapeDtypeStruct((rows, q.shape[1]), jnp.float32),
        in_specs=[vmem] * 6, out_specs=vmem,
    )(q, kv, segq.reshape(rows, 1), segk.reshape(1, -1), posq.reshape(rows, 1), posk.reshape(1, -1))


def layer(
    hidden_in,
    queries,
    keys_values,
    request_of_row,
    page_route,
    expert_ids,
    expert_weights,
    norm_gain,
    shared_gate_up,
    shared_down,
    expert_gate_up,
    expert_down,
):
    groups = lax.axis_size("req")
    columns = lax.axis_size("head")
    token_rows = hidden_in.shape[0]
    model_width = hidden_in.shape[1]
    page_rows = token_rows // groups
    group_ids = jnp.arange(groups, dtype=jnp.int32)
    page_dest = page_route.reshape(groups)
    matches = (page_dest[None, :] == group_ids[:, None]).astype(jnp.int32)
    dest_order = jnp.sum(matches * group_ids[None, :], axis=1)

    def by_dest(array_in):
        return jnp.take(array_in.reshape(groups, page_rows, array_in.shape[1]), dest_order, axis=0)

    moved_kv = lax.all_to_all(by_dest(keys_values), "req", split_axis=0, concat_axis=0, tiled=True)
    key_value_rows = moved_kv.reshape(token_rows, keys_values.shape[1])
    kv_piece = lax.all_gather(key_value_rows, "head", axis=0, tiled=True)
    widths = (hidden_in.shape[1], queries.shape[1])
    packed = jnp.concatenate((hidden_in, queries), axis=1)
    moved = lax.all_to_all(by_dest(packed), "req", split_axis=0, concat_axis=0, tiled=True)
    gate_own, down_own, moved = lax.optimization_barrier(
        (expert_gate_up[0], expert_down[0], moved)
    )
    upward_ring = [(i, (i + 1) % groups) for i in range(groups)]
    downward_ring = [(i, (i - 1) % groups) for i in range(groups)]
    half = gate_own.shape[1] // 2
    gate_below = lax.ppermute(gate_own, "req", upward_ring)
    down_below = lax.ppermute(down_own, "req", upward_ring)
    gate_above = lax.ppermute(gate_own, "req", downward_ring)
    down_above = lax.ppermute(down_own, "req", downward_ring)
    gate_far_low = lax.ppermute(gate_below[:, :half], "req", upward_ring)
    down_far_low = lax.ppermute(down_below[:half], "req", upward_ring)
    gate_far_high = lax.ppermute(gate_above[:, half:], "req", downward_ring)
    down_far_high = lax.ppermute(down_above[half:], "req", downward_ring)
    weight_sets = (
        (gate_own, down_own),
        (gate_below, down_below),
        (gate_above, down_above),
        (gate_far_low, down_far_low),
        (gate_far_high, down_far_high),
    )
    moved = moved.reshape(token_rows, sum(widths))
    resid = moved[:, : widths[0]]
    rows_of_queries = moved[:, widths[0] :]
    query_start = lax.axis_index("head") * token_rows
    segment_query = lax.dynamic_slice_in_dim(request_of_row, query_start, token_rows)
    position_query = query_start + jnp.arange(token_rows, dtype=jnp.int32)
    position_key = jnp.arange(kv_piece.shape[0], dtype=jnp.int32)
    context = attention(
        rows_of_queries, kv_piece, segment_query, request_of_row, position_query, position_key
    )
    mixed_rows = resid.astype(jnp.float32) + context
    mean_square = jnp.mean(mixed_rows * mixed_rows, axis=1, keepdims=True)
    normed = (mixed_rows * lax.rsqrt(mean_square + 1e-06) * norm_gain).astype(jnp.bfloat16)
    pair_expert = expert_ids.reshape(-1)
    hit_table = (pair_expert[:, None] == jnp.arange(EXPERTS, dtype=jnp.int32)[None, :]).astype(
        jnp.int32
    )
    ranks = jnp.sum((jnp.cumsum(hit_table, axis=0) - 1) * hit_table, axis=1)
    slot_of = pair_expert * SLOT + ranks
    slots_all = EXPERTS * SLOT
    placing = jnp.arange(slots_all, dtype=jnp.int32)[:, None] == slot_of[None, :]
    placing = jnp.any(placing.reshape(slots_all, token_rows, TOP), axis=2).astype(jnp.bfloat16)
    outgoing = jnp.dot(placing, normed, preferred_element_type=jnp.float32).astype(jnp.bfloat16)
    local_experts = expert_gate_up.shape[0]
    outgoing = outgoing.reshape(columns, local_experts * SLOT, model_width)
    shared_both = jnp.einsum(
        "td,dkf->tkf", normed, shared_gate_up, preferred_element_type=jnp.float32
    )
    shared_hidden = silu_mul(shared_both[:, 0], shared_both[:, 1]).astype(jnp.bfloat16)
    shared_out = jnp.dot(shared_hidden, shared_down, preferred_element_type=jnp.float32)
    arrived = lax.all_to_all(outgoing, "head", split_axis=0, concat_axis=0, tiled=True)
    expert_rows = arrived.reshape(-1, model_width)
    hidden_parts = []
    for gate_weights, _ in weight_sets:
        gate_value = jnp.dot(
            expert_rows, gate_weights[0].T, preferred_element_type=jnp.float32
        )
        upward = jnp.dot(expert_rows, gate_weights[1].T, preferred_element_type=jnp.float32)
        hidden_parts.append(silu_mul(gate_value, upward).astype(jnp.bfloat16))
    hidden_all = jnp.concatenate(hidden_parts, axis=1)
    down_all = jnp.concatenate([down_weights for _, down_weights in weight_sets], axis=0)
    out_rows = jnp.dot(hidden_all, down_all, preferred_element_type=jnp.float32)
    returned = lax.all_to_all(
        out_rows.astype(jnp.bfloat16).reshape(columns, local_experts * SLOT, model_width),
        "head",
        split_axis=0,
        concat_axis=0,
        tiled=True,
    )
    returned = returned.reshape(slots_all, model_width)
    picking = (slot_of[:, None] == jnp.arange(slots_all, dtype=jnp.int32)[None, :]).astype(
        jnp.bfloat16
    )
    pair_sum = jnp.dot(picking, returned, preferred_element_type=jnp.float32)
    pair_sum = pair_sum.reshape(token_rows, TOP, model_width)
    routed = jnp.sum(pair_sum * expert_weights[:, :, None], axis=1)
    return (mixed_rows + shared_out + routed).astype(jnp.bfloat16)


def solution(mesh):
    return jax.shard_map(
        layer,
        mesh=mesh,
        in_specs=(
            P(("req", "head"), None),
            P(("req", "head"), None),
            P(("req", "head"), None),
            P("req"),
            P("req", "head", None),
            P(("req", "head"), None),
            P(("req", "head"), None),
            P(),
            P(),
            P(),
            P("head", None, "req", None),
            P("head", "req", None),
        ),
        out_specs=P(("req", "head"), None),
        check_vma=False,
    )
```

```python
import functools

import jax
import jax.numpy as jnp
from jax import lax
from jax.experimental import pallas as pl
from jax.experimental.pallas import tpu as pltpu
from jax.sharding import PartitionSpec as P


EXPERTS = 32
TOP = 6
SLOT = 16


def silu_mul(gate_value, upward):
    return gate_value / (1.0 + jnp.exp(-gate_value)) * upward


def attn_kernel(q_ref, kv_ref, segq_ref, segk_ref, posq_ref, posk_ref, out_ref, *, heads, kv_heads, size):
    allowed = (segq_ref[...] == segk_ref[...]) & (posk_ref[...] <= posq_ref[...])
    frac = heads // kv_heads
    width = kv_heads * size
    for g in range(kv_heads):
        keys = kv_ref[:, g * size:(g + 1) * size]
        values = kv_ref[:, width + g * size: width + (g + 1) * size]
        for j in range(frac):
            h = g * frac + j
            qh = q_ref[:, h * size:(h + 1) * size]
            score = lax.dot_general(qh, keys, (((1,), (1,)), ((), ())), preferred_element_type=jnp.float32) * (size ** -0.5)
            masked = jnp.where(allowed, score, -1e30)
            top = jnp.max(masked, axis=1, keepdims=True)
            weights = jnp.where(allowed, jnp.exp(masked - top), 0.0)
            total = jnp.sum(weights, axis=1, keepdims=True)
            ctx = jnp.dot(weights.astype(jnp.bfloat16), values, preferred_element_type=jnp.float32)
            out_ref[:, h * size:(h + 1) * size] = ctx / total


def attention(q, kv, segq, segk, posq, posk):
    rows = q.shape[0]
    vmem = pl.BlockSpec(memory_space=pltpu.VMEM)
    return pl.pallas_call(
        functools.partial(attn_kernel, heads=16, kv_heads=4, size=128),
        out_shape=jax.ShapeDtypeStruct((rows, q.shape[1]), jnp.float32),
        in_specs=[vmem] * 6, out_specs=vmem,
    )(q, kv, segq.reshape(rows, 1), segk.reshape(1, -1), posq.reshape(rows, 1), posk.reshape(1, -1))


def layer(
    hidden_in,
    queries,
    keys_values,
    request_of_row,
    page_route,
    expert_ids,
    expert_weights,
    norm_gain,
    shared_gate_up,
    shared_down,
    expert_gate_up,
    expert_down,
):
    groups = lax.axis_size("req")
    columns = lax.axis_size("head")
    token_rows = hidden_in.shape[0]
    model_width = hidden_in.shape[1]
    page_rows = token_rows // groups
    group_ids = jnp.arange(groups, dtype=jnp.int32)
    page_dest = page_route.reshape(groups)
    matches = (page_dest[None, :] == group_ids[:, None]).astype(jnp.int32)
    dest_order = jnp.sum(matches * group_ids[None, :], axis=1)

    def by_dest(array_in):
        return jnp.take(array_in.reshape(groups, page_rows, array_in.shape[1]), dest_order, axis=0)

    widths = (hidden_in.shape[1], queries.shape[1], keys_values.shape[1])
    packed = jnp.concatenate((hidden_in, queries, keys_values), axis=1)
    moved = lax.all_to_all(by_dest(packed), "req", split_axis=0, concat_axis=0, tiled=True)
    gate_own, down_own, moved = lax.optimization_barrier(
        (expert_gate_up[0], expert_down[0], moved)
    )
    upward_ring = [(i, (i + 1) % groups) for i in range(groups)]
    downward_ring = [(i, (i - 1) % groups) for i in range(groups)]
    half = gate_own.shape[1] // 2
    gate_below = lax.ppermute(gate_own, "req", upward_ring)
    down_below = lax.ppermute(down_own, "req", upward_ring)
    gate_above = lax.ppermute(gate_own, "req", downward_ring)
    down_above = lax.ppermute(down_own, "req", downward_ring)
    gate_far_low = lax.ppermute(gate_below[:, :half], "req", upward_ring)
    down_far_low = lax.ppermute(down_below[:half], "req", upward_ring)
    gate_far_high = lax.ppermute(gate_above[:, half:], "req", downward_ring)
    down_far_high = lax.ppermute(down_above[half:], "req", downward_ring)
    weight_sets = (
        (gate_own, down_own),
        (gate_below, down_below),
        (gate_above, down_above),
        (gate_far_low, down_far_low),
        (gate_far_high, down_far_high),
    )
    moved = moved.reshape(token_rows, sum(widths))
    resid = moved[:, : widths[0]]
    rows_of_queries = moved[:, widths[0] : widths[0] + widths[1]]
    key_value_rows = moved[:, widths[0] + widths[1] :]
    kv_copies = jnp.broadcast_to(key_value_rows[None], (columns,) + key_value_rows.shape)
    kv_piece = lax.all_to_all(kv_copies, "head", split_axis=0, concat_axis=0, tiled=True)
    kv_piece = kv_piece.reshape(-1, key_value_rows.shape[1])
    query_start = lax.axis_index("head") * token_rows
    segment_query = lax.dynamic_slice_in_dim(request_of_row, query_start, token_rows)
    position_query = query_start + jnp.arange(token_rows, dtype=jnp.int32)
    position_key = jnp.arange(kv_piece.shape[0], dtype=jnp.int32)
    context = attention(
        rows_of_queries, kv_piece, segment_query, request_of_row, position_query, position_key
    )
    mixed_rows = resid.astype(jnp.float32) + context
    mean_square = jnp.mean(mixed_rows * mixed_rows, axis=1, keepdims=True)
    normed = (mixed_rows * lax.rsqrt(mean_square + 1e-06) * norm_gain).astype(jnp.bfloat16)
    pair_expert = expert_ids.reshape(-1)
    hit_table = (pair_expert[:, None] == jnp.arange(EXPERTS, dtype=jnp.int32)[None, :]).astype(
        jnp.int32
    )
    ranks = jnp.sum((jnp.cumsum(hit_table, axis=0) - 1) * hit_table, axis=1)
    slot_of = pair_expert * SLOT + ranks
    slots_all = EXPERTS * SLOT
    placing = jnp.arange(slots_all, dtype=jnp.int32)[:, None] == slot_of[None, :]
    placing = jnp.any(placing.reshape(slots_all, token_rows, TOP), axis=2).astype(jnp.bfloat16)
    outgoing = jnp.dot(placing, normed, preferred_element_type=jnp.float32).astype(jnp.bfloat16)
    local_experts = expert_gate_up.shape[0]
    outgoing = outgoing.reshape(columns, local_experts * SLOT, model_width)
    shared_both = jnp.einsum(
        "td,dkf->tkf", normed, shared_gate_up, preferred_element_type=jnp.float32
    )
    shared_hidden = silu_mul(shared_both[:, 0], shared_both[:, 1]).astype(jnp.bfloat16)
    shared_out = jnp.dot(shared_hidden, shared_down, preferred_element_type=jnp.float32)
    arrived = lax.all_to_all(outgoing, "head", split_axis=0, concat_axis=0, tiled=True)
    expert_rows = arrived.reshape(-1, model_width)
    hidden_parts = []
    for gate_weights, _ in weight_sets:
        gate_value = jnp.dot(
            expert_rows, gate_weights[0].T, preferred_element_type=jnp.float32
        )
        upward = jnp.dot(expert_rows, gate_weights[1].T, preferred_element_type=jnp.float32)
        hidden_parts.append(silu_mul(gate_value, upward).astype(jnp.bfloat16))
    hidden_all = jnp.concatenate(hidden_parts, axis=1)
    down_all = jnp.concatenate([down_weights for _, down_weights in weight_sets], axis=0)
    out_rows = jnp.dot(hidden_all, down_all, preferred_element_type=jnp.float32)
    returned = lax.all_to_all(
        out_rows.astype(jnp.bfloat16).reshape(columns, local_experts * SLOT, model_width),
        "head",
        split_axis=0,
        concat_axis=0,
        tiled=True,
    )
    returned = returned.reshape(slots_all, model_width)
    picking = (slot_of[:, None] == jnp.arange(slots_all, dtype=jnp.int32)[None, :]).astype(
        jnp.bfloat16
    )
    pair_sum = jnp.dot(picking, returned, preferred_element_type=jnp.float32)
    pair_sum = pair_sum.reshape(token_rows, TOP, model_width)
    routed = jnp.sum(pair_sum * expert_weights[:, :, None], axis=1)
    return (mixed_rows + shared_out + routed).astype(jnp.bfloat16)


def solution(mesh):
    return jax.shard_map(
        layer,
        mesh=mesh,
        in_specs=(
            P(("req", "head"), None),
            P(("req", "head"), None),
            P(("req", "head"), None),
            P("req"),
            P("req", "head", None),
            P(("req", "head"), None),
            P(("req", "head"), None),
            P(),
            P(),
            P(),
            P("head", None, "req", None),
            P("head", "req", None),
        ),
        out_specs=P(("req", "head"), None),
        check_vma=False,
    )
```

```python
import functools

import jax
import jax.numpy as jnp
from jax import lax
from jax.experimental import pallas as pl
from jax.experimental.pallas import tpu as pltpu
from jax.sharding import PartitionSpec as P


EXPERTS = 32
TOP = 6
SLOT = 16


def silu_mul(gate_value, upward):
    return gate_value / (1.0 + jnp.exp(-gate_value)) * upward


def attn_kernel(q_ref, kv_ref, segq_ref, segk_ref, posq_ref, posk_ref, out_ref, *, heads, kv_heads, size):
    allowed = (segq_ref[...] == segk_ref[...]) & (posk_ref[...] <= posq_ref[...])
    frac = heads // kv_heads
    width = kv_heads * size
    for g in range(kv_heads):
        keys = kv_ref[:, g * size:(g + 1) * size]
        values = kv_ref[:, width + g * size: width + (g + 1) * size]
        for j in range(frac):
            h = g * frac + j
            qh = q_ref[:, h * size:(h + 1) * size]
            score = lax.dot_general(qh, keys, (((1,), (1,)), ((), ())), preferred_element_type=jnp.float32) * (size ** -0.5)
            masked = jnp.where(allowed, score, -1e30)
            top = jnp.max(masked, axis=1, keepdims=True)
            weights = jnp.where(allowed, jnp.exp(masked - top), 0.0)
            total = jnp.sum(weights, axis=1, keepdims=True)
            ctx = jnp.dot(weights.astype(jnp.bfloat16), values, preferred_element_type=jnp.float32)
            out_ref[:, h * size:(h + 1) * size] = ctx / total


def attention(q, kv, segq, segk, posq, posk):
    rows = q.shape[0]
    vmem = pl.BlockSpec(memory_space=pltpu.VMEM)
    return pl.pallas_call(
        functools.partial(attn_kernel, heads=16, kv_heads=4, size=128),
        out_shape=jax.ShapeDtypeStruct((rows, q.shape[1]), jnp.float32),
        in_specs=[vmem] * 6, out_specs=vmem,
    )(q, kv, segq.reshape(rows, 1), segk.reshape(1, -1), posq.reshape(rows, 1), posk.reshape(1, -1))


def layer(
    hidden_in,
    queries,
    keys_values,
    request_of_row,
    page_route,
    expert_ids,
    expert_weights,
    norm_gain,
    shared_gate_up,
    shared_down,
    expert_gate_up,
    expert_down,
):
    groups = lax.axis_size("req")
    columns = lax.axis_size("head")
    token_rows = hidden_in.shape[0]
    model_width = hidden_in.shape[1]
    page_rows = token_rows // groups
    group_ids = jnp.arange(groups, dtype=jnp.int32)
    page_dest = page_route.reshape(groups)
    matches = (page_dest[None, :] == group_ids[:, None]).astype(jnp.int32)
    dest_order = jnp.sum(matches * group_ids[None, :], axis=1)

    def by_dest(array_in):
        return jnp.take(array_in.reshape(groups, page_rows, array_in.shape[1]), dest_order, axis=0)

    widths = (hidden_in.shape[1], queries.shape[1], keys_values.shape[1])
    packed = jnp.concatenate((hidden_in, queries, keys_values), axis=1)
    moved = lax.all_to_all(by_dest(packed), "req", split_axis=0, concat_axis=0, tiled=True)
    gate_own, down_own, moved = lax.optimization_barrier(
        (expert_gate_up[0], expert_down[0], moved)
    )
    upward_ring = [(i, (i + 1) % groups) for i in range(groups)]
    downward_ring = [(i, (i - 1) % groups) for i in range(groups)]
    half = gate_own.shape[1] // 2
    gate_below = lax.ppermute(gate_own, "req", upward_ring)
    down_below = lax.ppermute(down_own, "req", upward_ring)
    gate_above = lax.ppermute(gate_own, "req", downward_ring)
    down_above = lax.ppermute(down_own, "req", downward_ring)
    gate_far_low = lax.ppermute(gate_below[:, :half], "req", upward_ring)
    down_far_low = lax.ppermute(down_below[:half], "req", upward_ring)
    gate_far_high = lax.ppermute(gate_above[:, half:], "req", downward_ring)
    down_far_high = lax.ppermute(down_above[half:], "req", downward_ring)
    weight_sets = (
        (gate_own, down_own),
        (gate_below, down_below),
        (gate_above, down_above),
        (gate_far_low, down_far_low),
        (gate_far_high, down_far_high),
    )
    moved = moved.reshape(token_rows, sum(widths))
    resid = moved[:, : widths[0]]
    rows_of_queries = moved[:, widths[0] : widths[0] + widths[1]]
    key_value_rows = moved[:, widths[0] + widths[1] :]
    kv_copies = jnp.broadcast_to(key_value_rows[None], (columns,) + key_value_rows.shape)
    kv_piece = lax.all_to_all(kv_copies, "head", split_axis=0, concat_axis=0, tiled=True)
    kv_piece = kv_piece.reshape(-1, key_value_rows.shape[1])
    query_start = lax.axis_index("head") * token_rows
    segment_query = lax.dynamic_slice_in_dim(request_of_row, query_start, token_rows)
    position_query = query_start + jnp.arange(token_rows, dtype=jnp.int32)
    position_key = jnp.arange(kv_piece.shape[0], dtype=jnp.int32)
    context = attention(
        rows_of_queries, kv_piece, segment_query, request_of_row, position_query, position_key
    )
    mixed_rows = resid.astype(jnp.float32) + context
    mean_square = jnp.mean(mixed_rows * mixed_rows, axis=1, keepdims=True)
    normed = (mixed_rows * lax.rsqrt(mean_square + 1e-06) * norm_gain).astype(jnp.bfloat16)
    pair_expert = expert_ids.reshape(-1)
    hit_table = (pair_expert[:, None] == jnp.arange(EXPERTS, dtype=jnp.int32)[None, :]).astype(
        jnp.int32
    )
    ranks = jnp.sum((jnp.cumsum(hit_table, axis=0) - 1) * hit_table, axis=1)
    slot_of = pair_expert * SLOT + ranks
    slots_all = EXPERTS * SLOT
    placing = jnp.arange(slots_all, dtype=jnp.int32)[:, None] == slot_of[None, :]
    placing = jnp.any(placing.reshape(slots_all, token_rows, TOP), axis=2).astype(jnp.bfloat16)
    outgoing = jnp.dot(placing, normed, preferred_element_type=jnp.float32).astype(
        jnp.bfloat16
    )
    local_experts = expert_gate_up.shape[0]
    outgoing = outgoing.reshape(columns, local_experts * SLOT, model_width)
    shared_both = jnp.einsum(
        "td,dkf->tkf", normed, shared_gate_up, preferred_element_type=jnp.float32
    )
    shared_hidden = silu_mul(shared_both[:, 0], shared_both[:, 1]).astype(jnp.bfloat16)
    shared_out = jnp.dot(shared_hidden, shared_down, preferred_element_type=jnp.float32)
    arrived = lax.all_to_all(outgoing, "head", split_axis=0, concat_axis=0, tiled=True)
    expert_rows = arrived.reshape(-1, model_width)
    hidden_parts = []
    for sets in (weight_sets[:3], weight_sets[3:]):
        gate_matrix = jnp.concatenate([weights[0] for weights, _ in sets], axis=0)
        up_matrix = jnp.concatenate([weights[1] for weights, _ in sets], axis=0)
        gate_value = jnp.dot(expert_rows, gate_matrix.T, preferred_element_type=jnp.float32)
        upward = jnp.dot(expert_rows, up_matrix.T, preferred_element_type=jnp.float32)
        hidden_parts.append(silu_mul(gate_value, upward).astype(jnp.bfloat16))
    hidden_all = jnp.concatenate(hidden_parts, axis=1)
    down_all = jnp.concatenate([down_weights for _, down_weights in weight_sets], axis=0)
    out_rows = jnp.dot(hidden_all, down_all, preferred_element_type=jnp.float32)
    returned = lax.all_to_all(
        out_rows.astype(jnp.bfloat16).reshape(columns, local_experts * SLOT, model_width),
        "head",
        split_axis=0,
        concat_axis=0,
        tiled=True,
    )
    returned = returned.reshape(slots_all, model_width)
    picking = (slot_of[:, None] == jnp.arange(slots_all, dtype=jnp.int32)[None, :]).astype(
        jnp.bfloat16
    )
    pair_sum = jnp.dot(picking, returned, preferred_element_type=jnp.float32)
    pair_sum = pair_sum.reshape(token_rows, TOP, model_width)
    routed = jnp.sum(pair_sum * expert_weights[:, :, None], axis=1)
    return (mixed_rows + shared_out + routed).astype(jnp.bfloat16)


def solution(mesh):
    return jax.shard_map(
        layer,
        mesh=mesh,
        in_specs=(
            P(("req", "head"), None),
            P(("req", "head"), None),
            P(("req", "head"), None),
            P("req"),
            P("req", "head", None),
            P(("req", "head"), None),
            P(("req", "head"), None),
            P(),
            P(),
            P(),
            P("head", None, "req", None),
            P("head", "req", None),
        ),
        out_specs=P(("req", "head"), None),
        check_vma=False,
    )
```

```python
import functools

import jax
import jax.numpy as jnp
from jax import lax
from jax.experimental import pallas as pl
from jax.experimental.pallas import tpu as pltpu
from jax.sharding import PartitionSpec as P


EXPERTS = 32
TOP = 6
SLOT = 16


def silu_mul(gate_value, upward):
    return gate_value / (1.0 + jnp.exp(-gate_value)) * upward


def attn_kernel(q_ref, kv_ref, segq_ref, segk_ref, posq_ref, posk_ref, out_ref, *, heads, kv_heads, size):
    allowed = (segq_ref[...] == segk_ref[...]) & (posk_ref[...] <= posq_ref[...])
    frac = heads // kv_heads
    width = kv_heads * size
    for g in range(kv_heads):
        keys = kv_ref[:, g * size:(g + 1) * size]
        values = kv_ref[:, width + g * size: width + (g + 1) * size]
        for j in range(frac):
            h = g * frac + j
            qh = q_ref[:, h * size:(h + 1) * size]
            score = lax.dot_general(qh, keys, (((1,), (1,)), ((), ())), preferred_element_type=jnp.float32) * (size ** -0.5)
            masked = jnp.where(allowed, score, -1e30)
            top = jnp.max(masked, axis=1, keepdims=True)
            weights = jnp.where(allowed, jnp.exp(masked - top), 0.0)
            total = jnp.sum(weights, axis=1, keepdims=True)
            ctx = jnp.dot(weights.astype(jnp.bfloat16), values, preferred_element_type=jnp.float32)
            out_ref[:, h * size:(h + 1) * size] = ctx / total


def attention(q, kv, segq, segk, posq, posk):
    rows = q.shape[0]
    vmem = pl.BlockSpec(memory_space=pltpu.VMEM)
    return pl.pallas_call(
        functools.partial(attn_kernel, heads=16, kv_heads=4, size=128),
        out_shape=jax.ShapeDtypeStruct((rows, q.shape[1]), jnp.float32),
        in_specs=[vmem] * 6, out_specs=vmem,
    )(q, kv, segq.reshape(rows, 1), segk.reshape(1, -1), posq.reshape(rows, 1), posk.reshape(1, -1))


def layer(
    hidden_in,
    queries,
    keys_values,
    request_of_row,
    page_route,
    expert_ids,
    expert_weights,
    norm_gain,
    shared_gate_up,
    shared_down,
    expert_gate_up,
    expert_down,
):
    groups = lax.axis_size("req")
    columns = lax.axis_size("head")
    token_rows = hidden_in.shape[0]
    model_width = hidden_in.shape[1]
    page_rows = token_rows // groups
    group_ids = jnp.arange(groups, dtype=jnp.int32)
    page_dest = page_route.reshape(groups)
    matches = (page_dest[None, :] == group_ids[:, None]).astype(jnp.int32)
    dest_order = jnp.sum(matches * group_ids[None, :], axis=1)

    def by_dest(array_in):
        return jnp.take(array_in.reshape(groups, page_rows, array_in.shape[1]), dest_order, axis=0)

    widths = (hidden_in.shape[1], queries.shape[1], keys_values.shape[1])
    packed = jnp.concatenate((hidden_in, queries, keys_values), axis=1)
    moved = lax.all_to_all(by_dest(packed), "req", split_axis=0, concat_axis=0, tiled=True)
    gate_own, down_own, moved = lax.optimization_barrier(
        (expert_gate_up[0], expert_down[0], moved)
    )
    upward_ring = [(i, (i + 1) % groups) for i in range(groups)]
    downward_ring = [(i, (i - 1) % groups) for i in range(groups)]
    half = gate_own.shape[1] // 2
    halves = (
        (gate_own[:, :half], down_own[:half]),
        (gate_own[:, half:], down_own[half:]),
    )
    below, above = [], []
    for gate_half, down_half in halves:
        below.append(
            (
                lax.ppermute(gate_half, "req", upward_ring),
                lax.ppermute(down_half, "req", upward_ring),
            )
        )
        above.append(
            (
                lax.ppermute(gate_half, "req", downward_ring),
                lax.ppermute(down_half, "req", downward_ring),
            )
        )
    far_low = tuple(lax.ppermute(w, "req", upward_ring) for w in below[0])
    far_high = tuple(lax.ppermute(w, "req", downward_ring) for w in above[1])
    weight_sets = ((gate_own, down_own), below[0], below[1], above[0], above[1], far_low, far_high)
    moved = moved.reshape(token_rows, sum(widths))
    resid = moved[:, : widths[0]]
    rows_of_queries = moved[:, widths[0] : widths[0] + widths[1]]
    key_value_rows = moved[:, widths[0] + widths[1] :]
    kv_copies = jnp.broadcast_to(key_value_rows[None], (columns,) + key_value_rows.shape)
    kv_piece = lax.all_to_all(kv_copies, "head", split_axis=0, concat_axis=0, tiled=True)
    kv_piece = kv_piece.reshape(-1, key_value_rows.shape[1])
    query_start = lax.axis_index("head") * token_rows
    segment_query = lax.dynamic_slice_in_dim(request_of_row, query_start, token_rows)
    position_query = query_start + jnp.arange(token_rows, dtype=jnp.int32)
    position_key = jnp.arange(kv_piece.shape[0], dtype=jnp.int32)
    context = attention(
        rows_of_queries, kv_piece, segment_query, request_of_row, position_query, position_key
    )
    mixed_rows = resid.astype(jnp.float32) + context
    mean_square = jnp.mean(mixed_rows * mixed_rows, axis=1, keepdims=True)
    normed = (mixed_rows * lax.rsqrt(mean_square + 1e-06) * norm_gain).astype(jnp.bfloat16)
    pair_expert = expert_ids.reshape(-1)
    hit_table = (pair_expert[:, None] == jnp.arange(EXPERTS, dtype=jnp.int32)[None, :]).astype(
        jnp.int32
    )
    ranks = jnp.sum((jnp.cumsum(hit_table, axis=0) - 1) * hit_table, axis=1)
    slot_of = pair_expert * SLOT + ranks
    slots_all = EXPERTS * SLOT
    placing = jnp.arange(slots_all, dtype=jnp.int32)[:, None] == slot_of[None, :]
    placing = jnp.any(placing.reshape(slots_all, token_rows, TOP), axis=2).astype(jnp.bfloat16)
    outgoing = jnp.dot(placing, normed, preferred_element_type=jnp.float32).astype(jnp.bfloat16)
    local_experts = expert_gate_up.shape[0]
    outgoing = outgoing.reshape(columns, local_experts * SLOT, model_width)
    shared_both = jnp.einsum(
        "td,dkf->tkf", normed, shared_gate_up, preferred_element_type=jnp.float32
    )
    shared_hidden = silu_mul(shared_both[:, 0], shared_both[:, 1]).astype(jnp.bfloat16)
    shared_out = jnp.dot(shared_hidden, shared_down, preferred_element_type=jnp.float32)
    arrived = lax.all_to_all(outgoing, "head", split_axis=0, concat_axis=0, tiled=True)
    expert_rows = arrived.reshape(-1, model_width)
    hidden_parts = []
    for sets in (weight_sets[:5], weight_sets[5:]):
        gate_matrix = jnp.concatenate([weights[0] for weights, _ in sets], axis=0)
        up_matrix = jnp.concatenate([weights[1] for weights, _ in sets], axis=0)
        gate_value = jnp.dot(expert_rows, gate_matrix.T, preferred_element_type=jnp.float32)
        upward = jnp.dot(expert_rows, up_matrix.T, preferred_element_type=jnp.float32)
        hidden_parts.append(silu_mul(gate_value, upward).astype(jnp.bfloat16))
    hidden_all = jnp.concatenate(hidden_parts, axis=1)
    down_all = jnp.concatenate([down_weights for _, down_weights in weight_sets], axis=0)
    out_rows = jnp.dot(hidden_all, down_all, preferred_element_type=jnp.float32)
    returned = lax.all_to_all(
        out_rows.astype(jnp.bfloat16).reshape(columns, local_experts * SLOT, model_width),
        "head",
        split_axis=0,
        concat_axis=0,
        tiled=True,
    )
    returned = returned.reshape(slots_all, model_width)
    picking = (slot_of[:, None] == jnp.arange(slots_all, dtype=jnp.int32)[None, :]).astype(
        jnp.bfloat16
    )
    pair_sum = jnp.dot(picking, returned, preferred_element_type=jnp.float32)
    pair_sum = pair_sum.reshape(token_rows, TOP, model_width)
    routed = jnp.sum(pair_sum * expert_weights[:, :, None], axis=1)
    return (mixed_rows + shared_out + routed).astype(jnp.bfloat16)


def solution(mesh):
    return jax.shard_map(
        layer,
        mesh=mesh,
        in_specs=(
            P(("req", "head"), None),
            P(("req", "head"), None),
            P(("req", "head"), None),
            P("req"),
            P("req", "head", None),
            P(("req", "head"), None),
            P(("req", "head"), None),
            P(),
            P(),
            P(),
            P("head", None, "req", None),
            P("head", "req", None),
        ),
        out_specs=P(("req", "head"), None),
        check_vma=False,
    )
```
